256 devices in a mesh: sec: 8 (over z_lo, y), dev: 32 (over z_hi, x, core).
Axes of the slice: x: 4, y: 4, z: 8 (z_hi: 4, z_lo: 2; z = z_hi * 2 + z_lo), core: 2. Of those that a mesh axis runs over, the one named last changes fastest.
Arguments:
- sources: float32 [2, 8, 65536], P(None, None, ('sec', 'dev')), may hold values from -16 to 16
- positions: float32 [3, 65536], P(None, ('sec', 'dev')), may hold values from -0.5 to 18, as said below
- weights: float32 [65536], P(('sec', 'dev')), may hold values from 0.5 to 2
- wavenumbers: float32 [8], replicated, may hold values from 1 to 8
- directions: float32 [3, 128], replicated, may hold values from -1 to 1
- box_centers: float32 [3, 256], replicated, may hold values from -0.25 to 18
- group_centers: float32 [3, 32], replicated, may hold values from -0.25 to 18
- near_pairs: int32 [256, 2, 10], P(('sec', 'dev')), may hold values from 0 to 5, as said below
- pair_counts: int32 [256], P(('sec', 'dev')), may hold values from 3 to 10, as said below
- box_lists: int32 [256, 4], P(('sec', 'dev')), may hold values from 0 to 255, as said below
- group_lists: int32 [32, 2], replicated, may hold values from 0 to 31, as said below
Outputs:
- result: float32 [2, 8, 65536], P(None, None, ('sec', 'dev'))
- rayleigh: float32 [2, 8], replicated
The draws below stay inside these ranges and needn't reach their ends.
Inputs may be any that keep to these rules, and one draw needn't show every extreme that they name: `positions`: panels of leaf l lie within half a unit of a grid point of a 16 by 16 layered grid, leaves in order along it. `near_pairs`: row 0 holds leaves of the device's own box, row 1 leaves of its window; the first three pairs of every device take a source leaf of the box before, of the box after, and the target leaf itself. `pair_counts`: some device has all 10 pairs live. `box_lists`: A row holds distinct boxes, never the box itself or the ones just before and after it. `group_lists`: A row holds distinct groups other than the group itself.
All inputs are finite; a program needn't handle non-finite values.
Results may differ from the reference program's by a relative error of at most 0.0003.
Values sent between devices are 32-bit elements; how exact they have to be, the bound alone decides.
No kernel may reach another device: no remote copies, remote signals or barrier semaphores. Data moves between devices by JAX's collectives and lax.ppermute only.
A program may use at most 64 MiB of HBM per device.

```python
import math
import jax
import jax.numpy as jnp
from jax import lax

LEAF = 128
LEAVES = 2
F = 8
Q = 128
PAIRS_LEAF = 5
ML1 = 4
ML2 = 2
GROUP = 8
P_DEV = 256
PAIRS_MAX = 10
PANELS = 65536
GROUPS = 32
DEVICES = 256


def leaf_grid(leaf_ids):
    grid_column = (leaf_ids % 16).astype(jnp.float32)
    grid_row = (leaf_ids // 16 % 16).astype(jnp.float32)
    grid_layer = (leaf_ids // 256).astype(jnp.float32)
    return jnp.stack([grid_column, grid_row, grid_layer])


def draw_sources(key, part):
    panel_ramp = jnp.arange(PANELS, dtype=jnp.float32) / PANELS
    samples = jnp.clip(jax.random.normal(key, (2, F, PANELS), jnp.float32), -4.0, 4.0)
    return samples * (1.0 + 2.0 * panel_ramp)


def draw_positions(key, part):
    leaf_ids = jnp.arange(PANELS, dtype=jnp.int32) // LEAF
    jitter = jax.random.uniform(key, (3, PANELS), jnp.float32, -0.5, 0.5)
    return leaf_grid(leaf_ids) + jitter


def draw_box_centers(key, part):
    leaf_ids = jnp.arange(DEVICES, dtype=jnp.int32)[:, None] * LEAVES + jnp.arange(LEAVES, dtype=jnp.int32)[None, :]
    mean_xyz = jnp.mean(leaf_grid(leaf_ids), axis=2)
    return mean_xyz + jax.random.uniform(key, (3, DEVICES), jnp.float32, -0.25, 0.25)


def draw_group_centers(key, part):
    leaf_ids = jnp.arange(GROUPS, dtype=jnp.int32)[:, None] * (GROUP * LEAVES) + jnp.arange(GROUP * LEAVES, dtype=jnp.int32)[None, :]
    mean_xyz = jnp.mean(leaf_grid(leaf_ids), axis=2)
    return mean_xyz + jax.random.uniform(key, (3, GROUPS), jnp.float32, -0.25, 0.25)


def draw_near_pairs(key, part):
    subkeys = jax.random.split(jax.random.fold_in(key, 11), 4)
    targets = jax.random.randint(subkeys[0], (DEVICES, PAIRS_MAX), 0, LEAVES)
    anchors = jax.random.randint(subkeys[1], (DEVICES, PAIRS_MAX), 0, 3 * LEAVES)
    preceding = jax.random.randint(subkeys[2], (DEVICES,), 0, LEAVES)
    following = jax.random.randint(subkeys[3], (DEVICES,), 2 * LEAVES, 3 * LEAVES)
    anchors = anchors.at[:, 0].set(preceding).at[:, 1].set(following).at[:, 2].set(targets[:, 2] + LEAVES)
    return jnp.stack([targets, anchors], axis=1).astype(jnp.int32)


def draw_pair_counts(key, part):
    subkeys = jax.random.split(jax.random.fold_in(key, 23), 3)
    lowest = max(3, PAIRS_MAX // 4)
    counts = jax.random.randint(subkeys[0], (DEVICES,), lowest, PAIRS_MAX + 1)
    fullest = jax.random.randint(subkeys[1], (), 0, DEVICES)
    emptiest = (fullest + 1 + jax.random.randint(subkeys[2], (), 0, DEVICES - 1)) % DEVICES
    return counts.at[fullest].set(PAIRS_MAX).at[emptiest].set(lowest).astype(jnp.int32)


def draw_box_lists(key, part):
    subkeys = jax.random.split(jax.random.fold_in(key, 37), DEVICES)
    offsets = jax.vmap(lambda row_key: jax.random.permutation(row_key, DEVICES - 3)[:ML1])(subkeys) + 2
    return ((jnp.arange(DEVICES, dtype=jnp.int32)[:, None] + offsets) % DEVICES).astype(jnp.int32)


def draw_group_lists(key, part):
    subkeys = jax.random.split(jax.random.fold_in(key, 41), GROUPS)
    offsets = jax.vmap(lambda row_key: jax.random.permutation(row_key, GROUPS - 1)[:ML2])(subkeys) + 1
    return ((jnp.arange(GROUPS, dtype=jnp.int32)[:, None] + offsets) % GROUPS).astype(jnp.int32)


def block_levels(key, dims, cuts, least, high):
    level, own = 1.0, jax.random.fold_in(key, 6)
    for dim, blocks in cuts:
        draws = jnp.exp(jax.random.uniform(jax.random.fold_in(own, dim), (blocks,), jnp.float32, least / len(cuts), high / len(cuts)))
        level = level * jnp.repeat(draws, dims[dim] // blocks).reshape([-1 if axis == dim else 1 for axis in range(len(dims))])
    return level


def setup_inputs(seed: int = 0) -> dict:
    arg_keys = jax.random.split(jax.random.key(seed), 12)
    return {
        "sources": draw_sources(jax.random.fold_in(arg_keys[11], 71), 0),
        "positions": draw_positions(jax.random.fold_in(arg_keys[11], 71), 0),
        "weights": jnp.clip(jnp.exp(math.log(2.0) - 1.3862944 * jax.random.uniform(arg_keys[2], (PANELS,), jnp.float32) ** block_levels(arg_keys[2], (PANELS,), ((0, 256),), -0.2, 0.2)), 0.5, 2.0),
        "wavenumbers": jnp.clip(jnp.exp(jax.random.uniform(arg_keys[3], (F,), jnp.float32, math.log(1.0), math.log(8.0))), 1.0, 8.0),
        "directions": jnp.clip(jax.random.uniform(arg_keys[4], (3, Q), jnp.float32, -1.0, 1.0), -1.0, 1.0),
        "box_centers": draw_box_centers(jax.random.fold_in(arg_keys[11], 71), 0),
        "group_centers": draw_group_centers(jax.random.fold_in(arg_keys[11], 71), 0),
        "near_pairs": draw_near_pairs(jax.random.fold_in(arg_keys[11], 71), 0),
        "pair_counts": draw_pair_counts(jax.random.fold_in(arg_keys[11], 71), 0),
        "box_lists": draw_box_lists(jax.random.fold_in(arg_keys[11], 71), 0),
        "group_lists": draw_group_lists(jax.random.fold_in(arg_keys[11], 71), 0),
    }


SOFT = 0.1

def kernel_block(targets_xyz, sources_xyz, wave_numbers, reach_scale):
    offsets = targets_xyz[:, :, None] - sources_xyz[:, None, :]
    distance = jnp.sqrt(lax.optimization_barrier(jnp.sum(offsets * offsets, axis=0)) + SOFT * SOFT)
    amplitude = reach_scale / distance
    phases = wave_numbers[:, None, None] * distance[None, :, :]
    return (amplitude[None] * jnp.cos(phases), amplitude[None] * jnp.sin(phases))

def apply_block(kernel, values):
    real_kernel, imag_kernel = kernel
    highest = lax.Precision.HIGHEST
    real_real = jnp.einsum('fab,fb->fa', real_kernel, values[0], precision=highest)
    imag_imag = jnp.einsum('fab,fb->fa', imag_kernel, values[1], precision=highest)
    real_imag = jnp.einsum('fab,fb->fa', real_kernel, values[1], precision=highest)
    imag_real = jnp.einsum('fab,fb->fa', imag_kernel, values[0], precision=highest)
    return jnp.stack([real_real - imag_imag, real_imag + imag_real])

def upward(group_index, box_centers, group_centers, directions, wave_numbers, multipoles, radius_box, radius_group):
    children = group_index * GROUP + jnp.arange(GROUP, dtype=jnp.int32)
    parent_proxies = lax.dynamic_index_in_dim(group_centers, group_index, 1, keepdims=False)[:, None] + radius_group * directions
    child_proxies = box_centers[:, children][:, :, None] + radius_box * directions[:, None, :]
    kernels = jax.vmap(kernel_block, in_axes=(None, 1, None, None))(parent_proxies, child_proxies, wave_numbers, radius_group)
    return jax.vmap(apply_block)(kernels, multipoles[children]).sum(0) / math.sqrt(GROUP * Q)

def reference(sources, positions, weights, wavenumbers, directions, box_centers, group_centers, near_pairs, pair_counts, box_lists, group_lists):
    radius_box = 1.0 + 0.5 * LEAVES
    radius_group = 2.0 * radius_box
    weighted = sources * weights[None, None, :]

    def box_proxies(index):
        return lax.dynamic_index_in_dim(box_centers, index, 1, keepdims=False)[:, None] + radius_box * directions

    def outgoing(device):
        first_panel = (device * P_DEV).astype(jnp.int32)
        local_xyz = lax.dynamic_slice_in_dim(positions, first_panel, P_DEV, 1)
        local_values = lax.dynamic_slice_in_dim(weighted, first_panel, P_DEV, 2)
        kernel = kernel_block(box_proxies(device), local_xyz, wavenumbers, radius_box)
        return apply_block(kernel, local_values) / math.sqrt(P_DEV)
    box_multipoles = lax.map(outgoing, jnp.arange(DEVICES, dtype=jnp.int32))

    def group_outgoing(group_index):
        return upward(group_index, box_centers, group_centers, directions, wavenumbers, box_multipoles, radius_box, radius_group)
    group_multipoles = lax.map(group_outgoing, jnp.arange(GROUPS, dtype=jnp.int32))
    padded_values = jnp.pad(weighted, ((0, 0), (0, 0), (P_DEV, P_DEV)))
    padded_xyz = jnp.pad(positions, ((0, 0), (P_DEV, P_DEV)))

    def respond(device):
        first_panel = (device * P_DEV).astype(jnp.int32)
        window_xyz = lax.dynamic_slice_in_dim(padded_xyz, first_panel, 3 * P_DEV, 1)
        window_values = lax.dynamic_slice_in_dim(padded_values, first_panel, 3 * P_DEV, 2)
        local_xyz = lax.dynamic_slice_in_dim(positions, first_panel, P_DEV, 1)
        local_sources = lax.dynamic_slice_in_dim(sources, first_panel, P_DEV, 2)
        device_pairs = near_pairs[device]
        live_count = pair_counts[device]

        def near_step(near_total, pair_index):
            target_leaf = (device_pairs[0, pair_index] * LEAF).astype(jnp.int32)
            anchor_leaf = (device_pairs[1, pair_index] * LEAF).astype(jnp.int32)
            target_xyz = lax.dynamic_slice_in_dim(local_xyz, target_leaf, LEAF, 1)
            anchor_xyz = lax.dynamic_slice_in_dim(window_xyz, anchor_leaf, LEAF, 1)
            anchor_values = lax.dynamic_slice_in_dim(window_values, anchor_leaf, LEAF, 2)
            near_block = apply_block(kernel_block(target_xyz, anchor_xyz, wavenumbers, 1.0), anchor_values)
            near_block = jnp.where(pair_index < live_count, near_block, jnp.zeros_like(near_block))
            existing = lax.dynamic_slice_in_dim(near_total, target_leaf, LEAF, 2)
            return (lax.dynamic_update_slice_in_dim(near_total, existing + near_block, target_leaf, 2), None)
        near_total, _ = lax.scan(near_step, jnp.zeros((2, F, P_DEV), jnp.float32), jnp.arange(PAIRS_MAX, dtype=jnp.int32))
        own_proxies = box_proxies(device)
        source_boxes = box_lists[device]
        source_proxies = box_centers[:, source_boxes][:, :, None] + radius_box * directions[:, None, :]
        kernels = jax.vmap(kernel_block, in_axes=(None, 1, None, None))(own_proxies, source_proxies, wavenumbers, radius_box)
        incoming = jax.vmap(apply_block)(kernels, box_multipoles[source_boxes]).sum(0) / math.sqrt(ML1 * Q)
        parent = (device // GROUP).astype(jnp.int32)
        parent_proxies = lax.dynamic_index_in_dim(group_centers, parent, 1, keepdims=False)[:, None] + radius_group * directions
        source_groups = group_lists[parent]
        group_proxies = group_centers[:, source_groups][:, :, None] + radius_group * directions[:, None, :]
        group_kernels = jax.vmap(kernel_block, in_axes=(None, 1, None, None))(parent_proxies, group_proxies, wavenumbers, radius_group)
        group_local = jax.vmap(apply_block)(group_kernels, group_multipoles[source_groups]).sum(0) / math.sqrt(ML2 * Q)
        descended = apply_block(kernel_block(own_proxies, parent_proxies, wavenumbers, radius_group), group_local) / math.sqrt(Q)
        box_local = incoming + descended
        far_field = apply_block(kernel_block(local_xyz, own_proxies, wavenumbers, radius_box), box_local) / math.sqrt(Q)
        return 0.5 * local_sources + near_total / math.sqrt(LEAF * PAIRS_LEAF) + far_field
    pieces = lax.map(respond, jnp.arange(DEVICES, dtype=jnp.int32))
    result = jnp.transpose(pieces, (1, 2, 0, 3)).reshape(2, F, PANELS)
    denominator = lax.optimization_barrier(jnp.sum(sources[0] * sources[0] + sources[1] * sources[1], axis=-1)) + 1e-06
    real_sum = lax.optimization_barrier(jnp.sum(sources[0] * result[0] + sources[1] * result[1], axis=-1))
    imag_sum = lax.optimization_barrier(jnp.sum(sources[0] * result[1] - sources[1] * result[0], axis=-1))
    rayleigh = jnp.stack([real_sum / denominator, imag_sum / denominator])
    return (result, rayleigh)
```

```python
import functools
import math

import jax
import jax.numpy as jnp
from jax import lax
from jax.sharding import Mesh
from jax.sharding import PartitionSpec as P

LEAF = 128
LEAVES = 2
F = 8
Q = 128
PAIRS_LEAF = 5
ML1 = 4
ML2 = 2
GROUP = 8
P_DEV = 256
PAIRS_MAX = 10
SEC_DEV = ("sec_0", "sec_1", "dev_0", "dev_1", "dev_2")
DEV = ("dev_0", "dev_1", "dev_2")


SOFT = 0.1


def extended(value, sides, width):
    edges = {}
    for axis, dim in sides:
        devices, length = (lax.axis_size(axis), value.shape[dim])
        up = [(i, (i + 1) % devices) for i in range(devices - 1)]
        last = lax.slice_in_dim(value, length - width, length, axis=dim)
        first = lax.slice_in_dim(value, 0, width, axis=dim)
        edges[dim] = (
            lax.ppermute(last, axis, up),
            lax.ppermute(first, axis, [(b, a) for a, b in up]),
        )
    done = []
    for _, dim in sides:
        low, high = edges[dim]
        around = [(width, width) if d in done else (0, 0) for d in range(value.ndim)]
        value = jnp.concatenate([jnp.pad(low, around), value, jnp.pad(high, around)], axis=dim)
        done.append(dim)
    return value


def partner(block, axis, stride):
    count = lax.axis_size(axis)
    route = []
    for low in range(count):
        high = low | 1 << stride
        if high != low and high < count:
            route += [(low, high), (high, low)]
    return lax.ppermute(block, axis, route)


def side_by_side(arrays, axis, dim, along):
    widths = [a.shape[along] for a in arrays]
    both = jnp.concatenate(arrays, axis=along)
    whole = lax.all_gather(both, axis, axis=dim, tiled=True)
    return tuple(jnp.split(whole, [sum(widths[:k]) for k in range(1, len(widths))], axis=along))


STAGES = ("dev_0", "sec_0", "sec_1", "dev_1", "dev_2")


def staged_gather(block):
    value = block
    for axis in STAGES:
        count = lax.axis_size(axis)
        pieces = [value]
        for shift in range(1, count):
            route = [(i, (i + shift) % count) for i in range(count)]
            pieces.append(lax.ppermute(value, axis, route))
        value = jnp.stack(pieces)
    return value.reshape((-1,) + block.shape)


def slot_of(boxes):
    coords = {}
    rest = boxes
    for axis in reversed(SEC_DEV):
        count = lax.axis_size(axis)
        coords[axis] = rest % count
        rest = rest // count
    slot = jnp.zeros_like(boxes)
    for axis in reversed(STAGES):
        count = lax.axis_size(axis)
        shift = (lax.axis_index(axis) - coords[axis]) % count
        slot = slot * count + shift
    return slot


def over_axes(value, axes):
    return functools.reduce(lax.psum, axes, value)


def kernel_block(targets_xyz, sources_xyz, wave_numbers, reach_scale):
    offsets = targets_xyz[:, :, None] - sources_xyz[:, None, :]
    distance = jnp.sqrt(jnp.sum(offsets * offsets, axis=0) + SOFT * SOFT)
    amplitude = reach_scale / distance
    phases = wave_numbers[:, None, None] * distance[None, :, :]
    return (amplitude[None] * jnp.cos(phases), amplitude[None] * jnp.sin(phases))


def apply_block(kernel, values):
    real_kernel, imag_kernel = kernel
    highest = lax.Precision.HIGHEST
    real_real = jnp.einsum("fab,fb->fa", real_kernel, values[0], precision=highest)
    imag_imag = jnp.einsum("fab,fb->fa", imag_kernel, values[1], precision=highest)
    real_imag = jnp.einsum("fab,fb->fa", real_kernel, values[1], precision=highest)
    imag_real = jnp.einsum("fab,fb->fa", imag_kernel, values[0], precision=highest)
    return jnp.stack([real_real - imag_imag, real_imag + imag_real])


def apply_transposed(kernel, values):
    real_kernel, imag_kernel = kernel
    highest = lax.Precision.HIGHEST
    real_real = jnp.einsum("fba,fb->fa", real_kernel, values[0], precision=highest)
    imag_imag = jnp.einsum("fba,fb->fa", imag_kernel, values[1], precision=highest)
    real_imag = jnp.einsum("fba,fb->fa", real_kernel, values[1], precision=highest)
    imag_real = jnp.einsum("fba,fb->fa", imag_kernel, values[0], precision=highest)
    return jnp.stack([real_real - imag_imag, real_imag + imag_real])


def on_device(
    sources,
    positions,
    weights,
    wavenumbers,
    directions,
    box_centers,
    group_centers,
    near_pairs,
    pair_counts,
    box_lists,
    group_lists,
):
    radius_box = 1.0 + 0.5 * LEAVES
    radius_group = 2.0 * radius_box
    device_index = lax.axis_index(SEC_DEV)
    weighted = sources * weights[None, None, :]
    packed = jnp.concatenate([weighted.reshape(2 * F, P_DEV), positions], axis=0)
    window = extended(packed, ((SEC_DEV, 1),), P_DEV)
    window_values = window[: 2 * F].reshape(2, F, 3 * LEAVES, LEAF)
    window_xyz = window[2 * F :].reshape(3, 3 * LEAVES, LEAF)
    local_xyz = positions.reshape(3, LEAVES, LEAF)
    targets = near_pairs[0, 0]
    anchors = near_pairs[0, 1]
    live_count = pair_counts[0]
    pair_block = math.gcd(8, PAIRS_MAX)
    leaf_ids = jnp.arange(LEAVES, dtype=jnp.int32)
    pair_ids = jnp.arange(pair_block, dtype=jnp.int32)
    batched_kernel = jax.vmap(kernel_block, in_axes=(1, 1, None, None))
    batched_apply = jax.vmap(apply_block, in_axes=(0, 2), out_axes=2)

    def near_turn(turn_index, near_total):
        first_pair = turn_index * pair_block
        target_ids = lax.dynamic_slice_in_dim(targets, first_pair, pair_block)
        anchor_ids = lax.dynamic_slice_in_dim(anchors, first_pair, pair_block)
        kernels = batched_kernel(
            local_xyz[:, target_ids], window_xyz[:, anchor_ids], wavenumbers, 1.0
        )
        blocks = batched_apply(kernels, window_values[:, :, anchor_ids])
        live_rows = first_pair + pair_ids < live_count
        placing = ((target_ids[:, None] == leaf_ids[None, :]) & live_rows[:, None]).astype(
            jnp.float32
        )
        return near_total + jnp.einsum(
            "rfsa,sl->rfla", blocks, placing, precision=lax.Precision.HIGHEST
        )

    turn_count = (live_count + pair_block - 1) // pair_block
    near_total = lax.fori_loop(
        0, turn_count, near_turn, jnp.zeros((2, F, LEAVES, LEAF), jnp.float32)
    )
    near_total = near_total.reshape(2, F, P_DEV)
    own_center = lax.dynamic_index_in_dim(box_centers, device_index, 1, keepdims=False)
    own_proxies = own_center[:, None] + radius_box * directions
    outward = kernel_block(own_proxies, positions, wavenumbers, radius_box)
    own_multipole = apply_block(outward, weighted) / math.sqrt(P_DEV)
    parent = device_index // GROUP
    parent_proxies = (
        lax.dynamic_index_in_dim(group_centers, parent, 1, keepdims=False)[:, None]
        + radius_group * directions
    )
    source_groups = lax.dynamic_index_in_dim(group_lists, parent, 0, keepdims=False)
    contribution = apply_block(
        kernel_block(parent_proxies, own_proxies, wavenumbers, radius_group), own_multipole
    ) / math.sqrt(GROUP * Q)
    group_term = contribution
    for level_bit in range(GROUP.bit_length() - 1):
        group_term = group_term + partner(group_term, DEV, level_bit)
    share_width = Q // GROUP
    member_rank = device_index % GROUP
    share_piece = lax.dynamic_slice_in_dim(group_term, member_rank * share_width, share_width, 2)
    staged = staged_gather(jnp.concatenate([own_multipole, share_piece], axis=2))
    gathered, shares = staged[..., :Q], staged[..., Q:]
    source_boxes = box_lists[0]
    children = source_groups[:, None] * GROUP + jnp.arange(GROUP, dtype=jnp.int32)[None, :]
    source_multipoles = (
        shares[slot_of(children)]
        .transpose(0, 2, 3, 1, 4)
        .reshape(source_groups.shape[0], 2, F, Q)
    )
    source_proxies = box_centers[:, source_boxes][:, :, None] + radius_box * directions[:, None, :]
    kernels = jax.vmap(kernel_block, in_axes=(None, 1, None, None))(
        own_proxies, source_proxies, wavenumbers, radius_box
    )
    incoming = jax.vmap(apply_block)(kernels, gathered[slot_of(source_boxes)]).sum(0) / math.sqrt(ML1 * Q)
    group_proxies = (
        group_centers[:, source_groups][:, :, None] + radius_group * directions[:, None, :]
    )
    group_kernels = jax.vmap(kernel_block, in_axes=(None, 1, None, None))(
        parent_proxies, group_proxies, wavenumbers, radius_group
    )
    group_local = jax.vmap(apply_block)(group_kernels, source_multipoles).sum(0) / math.sqrt(
        ML2 * Q
    )
    descended = apply_block(
        kernel_block(own_proxies, parent_proxies, wavenumbers, radius_group), group_local
    ) / math.sqrt(Q)
    box_local = incoming + descended
    far_field = apply_transposed(outward, box_local) / math.sqrt(Q)
    result = 0.5 * sources + near_total / math.sqrt(LEAF * PAIRS_LEAF) + far_field
    real_sum = jnp.sum(sources[0] * result[0] + sources[1] * result[1], axis=-1)
    imag_sum = jnp.sum(sources[0] * result[1] - sources[1] * result[0], axis=-1)
    squares = jnp.sum(sources[0] * sources[0] + sources[1] * sources[1], axis=-1)
    sums = lax.psum(jnp.stack([real_sum, imag_sum, squares]), SEC_DEV)
    rayleigh = sums[:2] / (sums[2] + 1e-06)[None, :]
    return (result, rayleigh)


def solution(mesh):
    split = Mesh(mesh.devices.reshape(2, 4, 4, 4, 2), ("sec_0", "sec_1", "dev_0", "dev_1", "dev_2"))
    placed = (
        P(None, None, SEC_DEV),
        P(None, SEC_DEV),
        P(SEC_DEV),
        P(),
        P(),
        P(),
        P(),
        P(SEC_DEV, None, None),
        P(SEC_DEV),
        P(SEC_DEV, None),
        P(),
    )
    return jax.shard_map(
        on_device,
        mesh=split,
        in_specs=placed,
        out_specs=(P(None, None, SEC_DEV), P()),
        check_vma=False,
    )
```

```python
import functools
import math

import jax
import jax.numpy as jnp
from jax import lax
from jax.experimental import pallas as pl
from jax.experimental.pallas import tpu as pltpu
from jax.sharding import Mesh
from jax.sharding import PartitionSpec as P

LEAF = 128
LEAVES = 2
F = 8
Q = 128
PAIRS_LEAF = 5
ML1 = 4
ML2 = 2
GROUP = 8
P_DEV = 256
PAIRS_MAX = 10
SEC_DEV = ("sec_0", "sec_1", "dev_0", "dev_1", "dev_2")
DEV = ("dev_0", "dev_1", "dev_2")


SOFT = 0.1


def extended(value, sides, width):
    edges = {}
    for axis, dim in sides:
        devices, length = (lax.axis_size(axis), value.shape[dim])
        up = [(i, (i + 1) % devices) for i in range(devices - 1)]
        last = lax.slice_in_dim(value, length - width, length, axis=dim)
        first = lax.slice_in_dim(value, 0, width, axis=dim)
        edges[dim] = (
            lax.ppermute(last, axis, up),
            lax.ppermute(first, axis, [(b, a) for a, b in up]),
        )
    done = []
    for _, dim in sides:
        low, high = edges[dim]
        around = [(width, width) if d in done else (0, 0) for d in range(value.ndim)]
        value = jnp.concatenate([jnp.pad(low, around), value, jnp.pad(high, around)], axis=dim)
        done.append(dim)
    return value


def partner(block, axis, stride):
    count = lax.axis_size(axis)
    route = []
    for low in range(count):
        high = low | 1 << stride
        if high != low and high < count:
            route += [(low, high), (high, low)]
    return lax.ppermute(block, axis, route)


def side_by_side(arrays, axis, dim, along):
    widths = [a.shape[along] for a in arrays]
    both = jnp.concatenate(arrays, axis=along)
    whole = lax.all_gather(both, axis, axis=dim, tiled=True)
    return tuple(jnp.split(whole, [sum(widths[:k]) for k in range(1, len(widths))], axis=along))


STAGES = ("dev_0", "sec_0", "sec_1", "dev_1", "dev_2")


def staged_gather(block):
    value = block
    for axis in STAGES:
        count = lax.axis_size(axis)
        pieces = [value]
        for shift in range(1, count):
            route = [(i, (i + shift) % count) for i in range(count)]
            pieces.append(lax.ppermute(value, axis, route))
        value = jnp.stack(pieces)
    return value.reshape((-1,) + block.shape)


def slot_of(boxes):
    coords = {}
    rest = boxes
    for axis in reversed(SEC_DEV):
        count = lax.axis_size(axis)
        coords[axis] = rest % count
        rest = rest // count
    slot = jnp.zeros_like(boxes)
    for axis in reversed(STAGES):
        count = lax.axis_size(axis)
        shift = (lax.axis_index(axis) - coords[axis]) % count
        slot = slot * count + shift
    return slot


def over_axes(value, axes):
    return functools.reduce(lax.psum, axes, value)


def kernel_block(targets_xyz, sources_xyz, wave_numbers, reach_scale):
    offsets = targets_xyz[:, :, None] - sources_xyz[:, None, :]
    distance = jnp.sqrt(jnp.sum(offsets * offsets, axis=0) + SOFT * SOFT)
    amplitude = reach_scale / distance
    phases = wave_numbers[:, None, None] * distance[None, :, :]
    return (amplitude[None] * jnp.cos(phases), amplitude[None] * jnp.sin(phases))


def apply_block(kernel, values):
    real_kernel, imag_kernel = kernel
    highest = lax.Precision.HIGHEST
    real_real = jnp.einsum("fab,fb->fa", real_kernel, values[0], precision=highest)
    imag_imag = jnp.einsum("fab,fb->fa", imag_kernel, values[1], precision=highest)
    real_imag = jnp.einsum("fab,fb->fa", real_kernel, values[1], precision=highest)
    imag_real = jnp.einsum("fab,fb->fa", imag_kernel, values[0], precision=highest)
    return jnp.stack([real_real - imag_imag, real_imag + imag_real])


def apply_transposed(kernel, values):
    real_kernel, imag_kernel = kernel
    highest = lax.Precision.HIGHEST
    real_real = jnp.einsum("fba,fb->fa", real_kernel, values[0], precision=highest)
    imag_imag = jnp.einsum("fba,fb->fa", imag_kernel, values[1], precision=highest)
    real_imag = jnp.einsum("fba,fb->fa", real_kernel, values[1], precision=highest)
    imag_real = jnp.einsum("fba,fb->fa", imag_kernel, values[0], precision=highest)
    return jnp.stack([real_real - imag_imag, real_imag + imag_real])


def _apply_body(scale, waves_ref, tgt_ref, src_ref, val_ref, out_ref):
    targets = tgt_ref[0]
    sources = src_ref[0]
    squared = None
    for axis in range(3):
        offset = targets[:, axis : axis + 1] - sources[axis : axis + 1, :]
        squared = offset * offset if squared is None else squared + offset * offset
    distance = jnp.sqrt(squared + SOFT * SOFT)
    amplitude = scale / distance
    dims = (((1,), (1,)), ((), ()))
    highest = lax.Precision.HIGHEST
    for f in range(out_ref.shape[1]):
        phase = waves_ref[f] * distance
        real_kernel = amplitude * jnp.cos(phase)
        imag_kernel = amplitude * jnp.sin(phase)
        values = val_ref[0, f]
        real_part = lax.dot_general(values, real_kernel, dims, precision=highest, preferred_element_type=jnp.float32)
        imag_part = lax.dot_general(values, imag_kernel, dims, precision=highest, preferred_element_type=jnp.float32)
        out_ref[0, f, 0:1, :] = real_part[0:1] - imag_part[1:2]
        out_ref[0, f, 1:2, :] = real_part[1:2] + imag_part[0:1]


def apply_kernel(targets, sources, values, waves, scale):
    n, a, _ = targets.shape
    b = sources.shape[2]
    f = values.shape[1]
    return pl.pallas_call(
        functools.partial(_apply_body, scale),
        grid=(n,),
        in_specs=[
            pl.BlockSpec(memory_space=pltpu.SMEM),
            pl.BlockSpec((1, a, 3), lambda i: (i, 0, 0)),
            pl.BlockSpec((1, 3, b), lambda i: (i, 0, 0)),
            pl.BlockSpec((1, f, 2, b), lambda i: (i, 0, 0, 0)),
        ],
        out_specs=pl.BlockSpec((1, f, 2, a), lambda i: (i, 0, 0, 0)),
        out_shape=jax.ShapeDtypeStruct((n, f, 2, a), jnp.float32),
    )(waves, targets, sources, values)


def helmholtz(targets, sources, values, waves, scale):
    out = apply_kernel(
        jnp.swapaxes(targets, 1, 2), sources, jnp.swapaxes(values, 1, 2), waves, scale
    )
    return jnp.swapaxes(out, 1, 2)


def staged_sum(value):
    for axis in STAGES:
        count = lax.axis_size(axis)
        pieces = [value]
        for shift in range(1, count):
            route = [(i, (i + shift) % count) for i in range(count)]
            pieces.append(lax.ppermute(value, axis, route))
        stacked = jnp.stack(pieces)
        order = (lax.axis_index(axis) - jnp.arange(count, dtype=jnp.int32)) % count
        ordered = stacked[order]
        value = ordered[0]
        for j in range(1, count):
            value = value + ordered[j]
    return value


def on_device(
    sources,
    positions,
    weights,
    wavenumbers,
    directions,
    box_centers,
    group_centers,
    near_pairs,
    pair_counts,
    box_lists,
    group_lists,
):
    radius_box = 1.0 + 0.5 * LEAVES
    radius_group = 2.0 * radius_box
    device_index = lax.axis_index(SEC_DEV)
    weighted = sources * weights[None, None, :]
    packed = jnp.concatenate([weighted.reshape(2 * F, P_DEV), positions], axis=0)
    window = extended(packed, ((SEC_DEV, 1),), P_DEV)
    window_values = window[: 2 * F].reshape(2, F, 3 * LEAVES, LEAF)
    window_xyz = window[2 * F :].reshape(3, 3 * LEAVES, LEAF)
    local_xyz = positions.reshape(3, LEAVES, LEAF)
    targets = near_pairs[0, 0]
    anchors = near_pairs[0, 1]
    live_count = pair_counts[0]
    pair_ids = jnp.arange(PAIRS_MAX, dtype=jnp.int32)
    leaf_ids = jnp.arange(LEAVES, dtype=jnp.int32)
    live = (pair_ids < live_count).astype(jnp.float32)
    near_values = jnp.transpose(window_values[:, :, anchors], (2, 0, 1, 3)) * live[:, None, None, None]
    blocks = helmholtz(
        jnp.transpose(local_xyz[:, targets], (1, 0, 2)),
        jnp.transpose(window_xyz[:, anchors], (1, 0, 2)),
        near_values,
        wavenumbers,
        1.0,
    )
    placing = (targets[:, None] == leaf_ids[None, :]).astype(jnp.float32)
    near_total = jnp.einsum(
        "srfa,sl->rfla", blocks, placing, precision=lax.Precision.HIGHEST
    ).reshape(2, F, P_DEV)
    own_center = lax.dynamic_index_in_dim(box_centers, device_index, 1, keepdims=False)
    own_proxies = own_center[:, None] + radius_box * directions
    own_multipole = helmholtz(
        own_proxies[None], positions[None], weighted[None], wavenumbers, radius_box
    )[0] / math.sqrt(P_DEV)
    parent = device_index // GROUP
    parent_proxies = (
        lax.dynamic_index_in_dim(group_centers, parent, 1, keepdims=False)[:, None]
        + radius_group * directions
    )
    source_groups = lax.dynamic_index_in_dim(group_lists, parent, 0, keepdims=False)
    contribution = helmholtz(
        parent_proxies[None], own_proxies[None], own_multipole[None], wavenumbers, radius_group
    )[0] / math.sqrt(GROUP * Q)
    group_term = contribution
    for level_bit in range(GROUP.bit_length() - 1):
        group_term = group_term + partner(group_term, DEV, level_bit)
    share_width = Q // GROUP
    member_rank = device_index % GROUP
    share_piece = lax.dynamic_slice_in_dim(group_term, member_rank * share_width, share_width, 2)
    staged = staged_gather(jnp.concatenate([own_multipole, share_piece], axis=2))
    gathered, shares = staged[..., :Q], staged[..., Q:]
    source_boxes = box_lists[0]
    children = source_groups[:, None] * GROUP + jnp.arange(GROUP, dtype=jnp.int32)[None, :]
    source_multipoles = (
        shares[slot_of(children)]
        .transpose(0, 2, 3, 1, 4)
        .reshape(source_groups.shape[0], 2, F, Q)
    )
    source_proxies = box_centers[:, source_boxes][:, :, None] + radius_box * directions[:, None, :]
    incoming = helmholtz(
        jnp.broadcast_to(own_proxies, (source_boxes.shape[0],) + own_proxies.shape),
        jnp.transpose(source_proxies, (1, 0, 2)),
        gathered[slot_of(source_boxes)],
        wavenumbers,
        radius_box,
    ).sum(0) / math.sqrt(ML1 * Q)
    group_proxies = (
        group_centers[:, source_groups][:, :, None] + radius_group * directions[:, None, :]
    )
    group_local = helmholtz(
        jnp.broadcast_to(parent_proxies, (source_groups.shape[0],) + parent_proxies.shape),
        jnp.transpose(group_proxies, (1, 0, 2)),
        source_multipoles,
        wavenumbers,
        radius_group,
    ).sum(0) / math.sqrt(ML2 * Q)
    descended = helmholtz(
        own_proxies[None], parent_proxies[None], group_local[None], wavenumbers, radius_group
    )[0] / math.sqrt(Q)
    box_local = incoming + descended
    far_field = helmholtz(
        positions[None], own_proxies[None], box_local[None], wavenumbers, radius_box
    )[0] / math.sqrt(Q)
    result = 0.5 * sources + near_total / math.sqrt(LEAF * PAIRS_LEAF) + far_field
    real_sum = jnp.sum(sources[0] * result[0] + sources[1] * result[1], axis=-1)
    imag_sum = jnp.sum(sources[0] * result[1] - sources[1] * result[0], axis=-1)
    squares = jnp.sum(sources[0] * sources[0] + sources[1] * sources[1], axis=-1)
    sums = staged_sum(jnp.stack([real_sum, imag_sum, squares]))
    rayleigh = sums[:2] / (sums[2] + 1e-06)[None, :]
    return (result, rayleigh)


def solution(mesh):
    split = Mesh(mesh.devices.reshape(2, 4, 4, 4, 2), ("sec_0", "sec_1", "dev_0", "dev_1", "dev_2"))
    placed = (
        P(None, None, SEC_DEV),
        P(None, SEC_DEV),
        P(SEC_DEV),
        P(),
        P(),
        P(),
        P(),
        P(SEC_DEV, None, None),
        P(SEC_DEV),
        P(SEC_DEV, None),
        P(),
    )
    return jax.shard_map(
        on_device,
        mesh=split,
        in_specs=placed,
        out_specs=(P(None, None, SEC_DEV), P()),
        check_vma=False,
    )
```

```python
import functools
import math

import jax
import jax.numpy as jnp
from jax import lax
from jax.experimental import pallas as pl
from jax.experimental.pallas import tpu as pltpu
from jax.sharding import Mesh
from jax.sharding import PartitionSpec as P

LEAF = 128
LEAVES = 2
F = 8
Q = 128
PAIRS_LEAF = 5
ML1 = 4
ML2 = 2
GROUP = 8
P_DEV = 256
PAIRS_MAX = 10
SEC_DEV = ("sec_0", "sec_1", "dev_0", "dev_1", "dev_2")
DEV = ("dev_0", "dev_1", "dev_2")


SOFT = 0.1


def extended(value, sides, width):
    edges = {}
    for axis, dim in sides:
        devices, length = (lax.axis_size(axis), value.shape[dim])
        up = [(i, (i + 1) % devices) for i in range(devices - 1)]
        last = lax.slice_in_dim(value, length - width, length, axis=dim)
        first = lax.slice_in_dim(value, 0, width, axis=dim)
        edges[dim] = (
            lax.ppermute(last, axis, up),
            lax.ppermute(first, axis, [(b, a) for a, b in up]),
        )
    done = []
    for _, dim in sides:
        low, high = edges[dim]
        around = [(width, width) if d in done else (0, 0) for d in range(value.ndim)]
        value = jnp.concatenate([jnp.pad(low, around), value, jnp.pad(high, around)], axis=dim)
        done.append(dim)
    return value


def partner(block, axis, stride):
    count = lax.axis_size(axis)
    route = []
    for low in range(count):
        high = low | 1 << stride
        if high != low and high < count:
            route += [(low, high), (high, low)]
    return lax.ppermute(block, axis, route)


STAGES = ("dev_0", "sec_0", "sec_1", "dev_1", "dev_2")


def staged_gather(block, fillers):
    value = block
    done = []
    for stage, axis in enumerate(STAGES):
        count = lax.axis_size(axis)
        pieces = [value]
        for shift in range(1, count):
            route = [(i, (i + shift) % count) for i in range(count)]
            pieces.append(lax.ppermute(value, axis, route))
        done.append(fillers[stage]())
        value = jnp.stack(pieces)
    return value.reshape((-1,) + block.shape), done


def slot_of(boxes):
    coords = {}
    rest = boxes
    for axis in reversed(SEC_DEV):
        count = lax.axis_size(axis)
        coords[axis] = rest % count
        rest = rest // count
    slot = jnp.zeros_like(boxes)
    for axis in reversed(STAGES):
        count = lax.axis_size(axis)
        shift = (lax.axis_index(axis) - coords[axis]) % count
        slot = slot * count + shift
    return slot


def _apply_body(scale, waves_ref, tgt_ref, src_ref, val_ref, out_ref):
    targets = tgt_ref[0]
    sources = src_ref[0]
    squared = None
    for axis in range(3):
        offset = targets[:, axis : axis + 1] - sources[axis : axis + 1, :]
        squared = offset * offset if squared is None else squared + offset * offset
    distance = jnp.sqrt(squared + SOFT * SOFT)
    amplitude = scale / distance
    dims = (((1,), (1,)), ((), ()))
    highest = lax.Precision.HIGHEST
    for f in range(out_ref.shape[1]):
        phase = waves_ref[f] * distance
        real_kernel = amplitude * jnp.cos(phase)
        imag_kernel = amplitude * jnp.sin(phase)
        values = val_ref[0, f]
        real_part = lax.dot_general(values, real_kernel, dims, precision=highest, preferred_element_type=jnp.float32)
        imag_part = lax.dot_general(values, imag_kernel, dims, precision=highest, preferred_element_type=jnp.float32)
        out_ref[0, f, 0:1, :] = real_part[0:1] - imag_part[1:2]
        out_ref[0, f, 1:2, :] = real_part[1:2] + imag_part[0:1]


def apply_kernel(targets, sources, values, waves, scale):
    n, a, _ = targets.shape
    b = sources.shape[2]
    f = values.shape[1]
    return pl.pallas_call(
        functools.partial(_apply_body, scale),
        grid=(n,),
        in_specs=[
            pl.BlockSpec(memory_space=pltpu.SMEM),
            pl.BlockSpec((1, a, 3), lambda i: (i, 0, 0)),
            pl.BlockSpec((1, 3, b), lambda i: (i, 0, 0)),
            pl.BlockSpec((1, f, 2, b), lambda i: (i, 0, 0, 0)),
        ],
        out_specs=pl.BlockSpec((1, f, 2, a), lambda i: (i, 0, 0, 0)),
        out_shape=jax.ShapeDtypeStruct((n, f, 2, a), jnp.float32),
    )(waves, targets, sources, values)


def helmholtz(targets, sources, values, waves, scale):
    out = apply_kernel(
        jnp.swapaxes(targets, 1, 2), sources, jnp.swapaxes(values, 1, 2), waves, scale
    )
    return jnp.swapaxes(out, 1, 2)


def staged_sum(value):
    for axis in STAGES:
        count = lax.axis_size(axis)
        pieces = [value]
        for shift in range(1, count):
            route = [(i, (i + shift) % count) for i in range(count)]
            pieces.append(lax.ppermute(value, axis, route))
        stacked = jnp.stack(pieces)
        order = (lax.axis_index(axis) - jnp.arange(count, dtype=jnp.int32)) % count
        ordered = stacked[order]
        value = ordered[0]
        for j in range(1, count):
            value = value + ordered[j]
    return value


def device_body(
    sources,
    positions,
    weights,
    wavenumbers,
    directions,
    box_centers,
    group_centers,
    near_pairs,
    pair_counts,
    box_lists,
    group_lists,
):
    radius_box = 1.0 + 0.5 * LEAVES
    radius_group = 2.0 * radius_box
    device_index = lax.axis_index(SEC_DEV)
    weighted = sources * weights[None, None, :]
    packed = jnp.concatenate([weighted.reshape(2 * F, P_DEV), positions], axis=0)
    window = extended(packed, ((SEC_DEV, 1),), P_DEV)
    window_values = window[: 2 * F].reshape(2, F, 3 * LEAVES, LEAF)
    window_xyz = window[2 * F :].reshape(3, 3 * LEAVES, LEAF)
    local_xyz = positions.reshape(3, LEAVES, LEAF)
    targets = near_pairs[0, 0]
    anchors = near_pairs[0, 1]
    live_count = pair_counts[0]
    pair_ids = jnp.arange(PAIRS_MAX, dtype=jnp.int32)
    leaf_ids = jnp.arange(LEAVES, dtype=jnp.int32)
    live = (pair_ids < live_count).astype(jnp.float32)
    near_values = jnp.transpose(window_values[:, :, anchors], (2, 0, 1, 3)) * live[:, None, None, None]
    near_targets = jnp.transpose(local_xyz[:, targets], (1, 0, 2))
    near_sources = jnp.transpose(window_xyz[:, anchors], (1, 0, 2))
    chunk = -(-PAIRS_MAX // len(STAGES))

    def near_part(first):
        def run():
            picked = slice(first, min(first + chunk, PAIRS_MAX))
            return helmholtz(
                near_targets[picked], near_sources[picked], near_values[picked], wavenumbers, 1.0
            )

        return run

    fillers = [near_part(k * chunk) for k in range(len(STAGES))]
    own_center = lax.dynamic_index_in_dim(box_centers, device_index, 1, keepdims=False)
    own_proxies = own_center[:, None] + radius_box * directions
    own_multipole = helmholtz(
        own_proxies[None], positions[None], weighted[None], wavenumbers, radius_box
    )[0] / math.sqrt(P_DEV)
    parent = device_index // GROUP
    parent_proxies = (
        lax.dynamic_index_in_dim(group_centers, parent, 1, keepdims=False)[:, None]
        + radius_group * directions
    )
    source_groups = lax.dynamic_index_in_dim(group_lists, parent, 0, keepdims=False)
    contribution = helmholtz(
        parent_proxies[None], own_proxies[None], own_multipole[None], wavenumbers, radius_group
    )[0] / math.sqrt(GROUP * Q)
    group_term = contribution
    for level_bit in range(GROUP.bit_length() - 1):
        group_term = group_term + partner(group_term, DEV, level_bit)
    share_width = Q // GROUP
    member_rank = device_index % GROUP
    share_piece = lax.dynamic_slice_in_dim(group_term, member_rank * share_width, share_width, 2)
    staged, parts = staged_gather(jnp.concatenate([own_multipole, share_piece], axis=2), fillers)
    blocks = jnp.concatenate(parts, axis=0)
    placing = (targets[:, None] == leaf_ids[None, :]).astype(jnp.float32)
    near_total = jnp.einsum(
        "srfa,sl->rfla", blocks, placing, precision=lax.Precision.HIGHEST
    ).reshape(2, F, P_DEV)
    gathered, shares = staged[..., :Q], staged[..., Q:]
    source_boxes = box_lists[0]
    children = source_groups[:, None] * GROUP + jnp.arange(GROUP, dtype=jnp.int32)[None, :]
    source_multipoles = (
        shares[slot_of(children)]
        .transpose(0, 2, 3, 1, 4)
        .reshape(source_groups.shape[0], 2, F, Q)
    )
    source_proxies = box_centers[:, source_boxes][:, :, None] + radius_box * directions[:, None, :]
    incoming = helmholtz(
        jnp.broadcast_to(own_proxies, (source_boxes.shape[0],) + own_proxies.shape),
        jnp.transpose(source_proxies, (1, 0, 2)),
        gathered[slot_of(source_boxes)],
        wavenumbers,
        radius_box,
    ).sum(0) / math.sqrt(ML1 * Q)
    group_proxies = (
        group_centers[:, source_groups][:, :, None] + radius_group * directions[:, None, :]
    )
    group_local = helmholtz(
        jnp.broadcast_to(parent_proxies, (source_groups.shape[0],) + parent_proxies.shape),
        jnp.transpose(group_proxies, (1, 0, 2)),
        source_multipoles,
        wavenumbers,
        radius_group,
    ).sum(0) / math.sqrt(ML2 * Q)
    descended = helmholtz(
        own_proxies[None], parent_proxies[None], group_local[None], wavenumbers, radius_group
    )[0] / math.sqrt(Q)
    box_local = incoming + descended
    far_field = helmholtz(
        positions[None], own_proxies[None], box_local[None], wavenumbers, radius_box
    )[0] / math.sqrt(Q)
    result = 0.5 * sources + near_total / math.sqrt(LEAF * PAIRS_LEAF) + far_field
    real_sum = jnp.sum(sources[0] * result[0] + sources[1] * result[1], axis=-1)
    imag_sum = jnp.sum(sources[0] * result[1] - sources[1] * result[0], axis=-1)
    squares = jnp.sum(sources[0] * sources[0] + sources[1] * sources[1], axis=-1)
    sums = staged_sum(jnp.stack([real_sum, imag_sum, squares]))
    rayleigh = sums[:2] / (sums[2] + 1e-06)[None, :]
    return (result, rayleigh)


def solution(mesh):
    split = Mesh(mesh.devices.reshape(2, 4, 4, 4, 2), ("sec_0", "sec_1", "dev_0", "dev_1", "dev_2"))
    placed = (
        P(None, None, SEC_DEV),
        P(None, SEC_DEV),
        P(SEC_DEV),
        P(),
        P(),
        P(),
        P(),
        P(SEC_DEV, None, None),
        P(SEC_DEV),
        P(SEC_DEV, None),
        P(),
    )
    return jax.shard_map(
        device_body,
        mesh=split,
        in_specs=placed,
        out_specs=(P(None, None, SEC_DEV), P()),
        check_vma=False,
    )
```

```python
import functools
import math

import jax
import jax.numpy as jnp
from jax import lax
from jax.experimental import pallas as pl
from jax.experimental.pallas import tpu as pltpu
from jax.sharding import Mesh
from jax.sharding import PartitionSpec as P

LEAF = 128
LEAVES = 2
F = 8
Q = 128
PAIRS_LEAF = 5
ML1 = 4
ML2 = 2
GROUP = 8
P_DEV = 256
PAIRS_MAX = 10
SEC_DEV = ("sec_0", "sec_1", "dev_0", "dev_1", "dev_2")
DEV = ("dev_0", "dev_1", "dev_2")


SOFT = 0.1


def extended(value, sides, width):
    edges = {}
    for axis, dim in sides:
        devices, length = (lax.axis_size(axis), value.shape[dim])
        up = [(i, (i + 1) % devices) for i in range(devices - 1)]
        last = lax.slice_in_dim(value, length - width, length, axis=dim)
        first = lax.slice_in_dim(value, 0, width, axis=dim)
        edges[dim] = (
            lax.ppermute(last, axis, up),
            lax.ppermute(first, axis, [(b, a) for a, b in up]),
        )
    done = []
    for _, dim in sides:
        low, high = edges[dim]
        around = [(width, width) if d in done else (0, 0) for d in range(value.ndim)]
        value = jnp.concatenate([jnp.pad(low, around), value, jnp.pad(high, around)], axis=dim)
        done.append(dim)
    return value


def partner(block, axis, stride):
    count = lax.axis_size(axis)
    route = []
    for low in range(count):
        high = low | 1 << stride
        if high != low and high < count:
            route += [(low, high), (high, low)]
    return lax.ppermute(block, axis, route)


STAGES = ("dev_0", "sec_0", "sec_1", "dev_1", "dev_2")


def staged_gather(block, fillers):
    value = block
    done = []
    for stage, axis in enumerate(STAGES):
        count = lax.axis_size(axis)
        pieces = [value]
        for shift in range(1, count):
            route = [(i, (i + shift) % count) for i in range(count)]
            pieces.append(lax.ppermute(value, axis, route))
        done.append(fillers[stage]())
        value = jnp.stack(pieces)
    return value.reshape((-1,) + block.shape), done


def slot_of(boxes):
    coords = {}
    rest = boxes
    for axis in reversed(SEC_DEV):
        count = lax.axis_size(axis)
        coords[axis] = rest % count
        rest = rest // count
    slot = jnp.zeros_like(boxes)
    for axis in reversed(STAGES):
        count = lax.axis_size(axis)
        shift = (lax.axis_index(axis) - coords[axis]) % count
        slot = slot * count + shift
    return slot


TWO_OVER_PI = 0.6366197723675814
PIO2_1 = 1.5703125
PIO2_2 = 4.837512969970703125e-4
PIO2_3 = 7.54978995489188216e-8


def sincos(x):
    turns = jnp.round(x * TWO_OVER_PI)
    r = ((x - turns * PIO2_1) - turns * PIO2_2) - turns * PIO2_3
    z = r * r
    s = r + r * z * (-1.6666654611e-1 + z * (8.3321608736e-3 + z * -1.9515295891e-4))
    c = 1.0 - 0.5 * z + z * z * (
        4.166664568298827e-2 + z * (-1.388731625493765e-3 + z * 2.443315711809948e-5)
    )
    quadrant = turns.astype(jnp.int32) & 3
    swap = (quadrant & 1) == 1
    sin_v = jnp.where(swap, c, s)
    cos_v = jnp.where(swap, s, c)
    sin_v = jnp.where(quadrant >= 2, -sin_v, sin_v)
    cos_v = jnp.where((quadrant == 1) | (quadrant == 2), -cos_v, cos_v)
    return sin_v, cos_v


def _apply_body(scale, waves_ref, tgt_ref, src_ref, val_ref, out_ref):
    targets = tgt_ref[0]
    sources = src_ref[0]
    squared = None
    for axis in range(3):
        offset = targets[:, axis : axis + 1] - sources[axis : axis + 1, :]
        squared = offset * offset if squared is None else squared + offset * offset
    distance = jnp.sqrt(squared + SOFT * SOFT)
    amplitude = scale / distance
    dims = (((1,), (1,)), ((), ()))
    highest = lax.Precision.HIGHEST
    for f in range(out_ref.shape[1]):
        phase = waves_ref[f] * distance
        sin_v, cos_v = sincos(phase)
        real_kernel = amplitude * cos_v
        imag_kernel = amplitude * sin_v
        values = val_ref[0, f]
        real_part = lax.dot_general(values, real_kernel, dims, precision=highest, preferred_element_type=jnp.float32)
        imag_part = lax.dot_general(values, imag_kernel, dims, precision=highest, preferred_element_type=jnp.float32)
        out_ref[0, f, 0:1, :] = real_part[0:1] - imag_part[1:2]
        out_ref[0, f, 1:2, :] = real_part[1:2] + imag_part[0:1]


def apply_kernel(targets, sources, values, waves, scale):
    n, a, _ = targets.shape
    b = sources.shape[2]
    f = values.shape[1]
    return pl.pallas_call(
        functools.partial(_apply_body, scale),
        grid=(n,),
        in_specs=[
            pl.BlockSpec(memory_space=pltpu.SMEM),
            pl.BlockSpec((1, a, 3), lambda i: (i, 0, 0)),
            pl.BlockSpec((1, 3, b), lambda i: (i, 0, 0)),
            pl.BlockSpec((1, f, 2, b), lambda i: (i, 0, 0, 0)),
        ],
        out_specs=pl.BlockSpec((1, f, 2, a), lambda i: (i, 0, 0, 0)),
        out_shape=jax.ShapeDtypeStruct((n, f, 2, a), jnp.float32),
    )(waves, targets, sources, values)


def helmholtz(targets, sources, values, waves, scale):
    out = apply_kernel(
        jnp.swapaxes(targets, 1, 2), sources, jnp.swapaxes(values, 1, 2), waves, scale
    )
    return jnp.swapaxes(out, 1, 2)


def staged_sum(value):
    for axis in STAGES:
        count = lax.axis_size(axis)
        pieces = [value]
        for shift in range(1, count):
            route = [(i, (i + shift) % count) for i in range(count)]
            pieces.append(lax.ppermute(value, axis, route))
        stacked = jnp.stack(pieces)
        order = (lax.axis_index(axis) - jnp.arange(count, dtype=jnp.int32)) % count
        ordered = stacked[order]
        value = ordered[0]
        for j in range(1, count):
            value = value + ordered[j]
    return value


def device_body(
    sources,
    positions,
    weights,
    wavenumbers,
    directions,
    box_centers,
    group_centers,
    near_pairs,
    pair_counts,
    box_lists,
    group_lists,
):
    radius_box = 1.0 + 0.5 * LEAVES
    radius_group = 2.0 * radius_box
    device_index = lax.axis_index(SEC_DEV)
    weighted = sources * weights[None, None, :]
    packed = jnp.concatenate([weighted.reshape(2 * F, P_DEV), positions], axis=0)
    window = extended(packed, ((SEC_DEV, 1),), P_DEV)
    window_values = window[: 2 * F].reshape(2, F, 3 * LEAVES, LEAF)
    window_xyz = window[2 * F :].reshape(3, 3 * LEAVES, LEAF)
    local_xyz = positions.reshape(3, LEAVES, LEAF)
    targets = near_pairs[0, 0]
    anchors = near_pairs[0, 1]
    live_count = pair_counts[0]
    pair_ids = jnp.arange(PAIRS_MAX, dtype=jnp.int32)
    leaf_ids = jnp.arange(LEAVES, dtype=jnp.int32)
    live = (pair_ids < live_count).astype(jnp.float32)
    near_values = jnp.transpose(window_values[:, :, anchors], (2, 0, 1, 3)) * live[:, None, None, None]
    near_targets = jnp.transpose(local_xyz[:, targets], (1, 0, 2))
    near_sources = jnp.transpose(window_xyz[:, anchors], (1, 0, 2))
    chunk = -(-PAIRS_MAX // len(STAGES))

    def near_part(first):
        def run():
            picked = slice(first, min(first + chunk, PAIRS_MAX))
            return helmholtz(
                near_targets[picked], near_sources[picked], near_values[picked], wavenumbers, 1.0
            )

        return run

    fillers = [near_part(k * chunk) for k in range(len(STAGES))]
    own_center = lax.dynamic_index_in_dim(box_centers, device_index, 1, keepdims=False)
    own_proxies = own_center[:, None] + radius_box * directions
    own_multipole = helmholtz(
        own_proxies[None], positions[None], weighted[None], wavenumbers, radius_box
    )[0] / math.sqrt(P_DEV)
    parent = device_index // GROUP
    parent_proxies = (
        lax.dynamic_index_in_dim(group_centers, parent, 1, keepdims=False)[:, None]
        + radius_group * directions
    )
    source_groups = lax.dynamic_index_in_dim(group_lists, parent, 0, keepdims=False)
    contribution = helmholtz(
        parent_proxies[None], own_proxies[None], own_multipole[None], wavenumbers, radius_group
    )[0] / math.sqrt(GROUP * Q)
    group_term = contribution
    for level_bit in range(GROUP.bit_length() - 1):
        group_term = group_term + partner(group_term, DEV, level_bit)
    share_width = Q // GROUP
    member_rank = device_index % GROUP
    share_piece = lax.dynamic_slice_in_dim(group_term, member_rank * share_width, share_width, 2)
    staged, parts = staged_gather(jnp.concatenate([own_multipole, share_piece], axis=2), fillers)
    blocks = jnp.concatenate(parts, axis=0)
    placing = (targets[:, None] == leaf_ids[None, :]).astype(jnp.float32)
    near_total = jnp.einsum(
        "srfa,sl->rfla", blocks, placing, precision=lax.Precision.HIGHEST
    ).reshape(2, F, P_DEV)
    gathered, shares = staged[..., :Q], staged[..., Q:]
    source_boxes = box_lists[0]
    children = source_groups[:, None] * GROUP + jnp.arange(GROUP, dtype=jnp.int32)[None, :]
    source_multipoles = (
        shares[slot_of(children)]
        .transpose(0, 2, 3, 1, 4)
        .reshape(source_groups.shape[0], 2, F, Q)
    )
    source_proxies = box_centers[:, source_boxes][:, :, None] + radius_box * directions[:, None, :]
    incoming = helmholtz(
        jnp.broadcast_to(own_proxies, (source_boxes.shape[0],) + own_proxies.shape),
        jnp.transpose(source_proxies, (1, 0, 2)),
        gathered[slot_of(source_boxes)],
        wavenumbers,
        radius_box,
    ).sum(0) / math.sqrt(ML1 * Q)
    group_proxies = (
        group_centers[:, source_groups][:, :, None] + radius_group * directions[:, None, :]
    )
    group_local = helmholtz(
        jnp.broadcast_to(parent_proxies, (source_groups.shape[0],) + parent_proxies.shape),
        jnp.transpose(group_proxies, (1, 0, 2)),
        source_multipoles,
        wavenumbers,
        radius_group,
    ).sum(0) / math.sqrt(ML2 * Q)
    descended = helmholtz(
        own_proxies[None], parent_proxies[None], group_local[None], wavenumbers, radius_group
    )[0] / math.sqrt(Q)
    box_local = incoming + descended
    far_field = helmholtz(
        positions[None], own_proxies[None], box_local[None], wavenumbers, radius_box
    )[0] / math.sqrt(Q)
    result = 0.5 * sources + near_total / math.sqrt(LEAF * PAIRS_LEAF) + far_field
    real_sum = jnp.sum(sources[0] * result[0] + sources[1] * result[1], axis=-1)
    imag_sum = jnp.sum(sources[0] * result[1] - sources[1] * result[0], axis=-1)
    squares = jnp.sum(sources[0] * sources[0] + sources[1] * sources[1], axis=-1)
    sums = staged_sum(jnp.stack([real_sum, imag_sum, squares]))
    rayleigh = sums[:2] / (sums[2] + 1e-06)[None, :]
    return (result, rayleigh)


def solution(mesh):
    split = Mesh(mesh.devices.reshape(2, 4, 4, 4, 2), ("sec_0", "sec_1", "dev_0", "dev_1", "dev_2"))
    placed = (
        P(None, None, SEC_DEV),
        P(None, SEC_DEV),
        P(SEC_DEV),
        P(),
        P(),
        P(),
        P(),
        P(SEC_DEV, None, None),
        P(SEC_DEV),
        P(SEC_DEV, None),
        P(),
    )
    return jax.shard_map(
        device_body,
        mesh=split,
        in_specs=placed,
        out_specs=(P(None, None, SEC_DEV), P()),
        check_vma=False,
    )
```

```python
import functools
import math

import jax
import jax.numpy as jnp
from jax import lax
from jax.experimental import pallas as pl
from jax.experimental.pallas import tpu as pltpu
from jax.sharding import Mesh
from jax.sharding import PartitionSpec as P

LEAF = 128
LEAVES = 2
F = 8
Q = 128
PAIRS_LEAF = 5
ML1 = 4
ML2 = 2
GROUP = 8
P_DEV = 256
PAIRS_MAX = 10
SEC_DEV = ("sec_0", "sec_1", "dev_0", "dev_1", "dev_2")
DEV = ("dev_0", "dev_1", "dev_2")


SOFT = 0.1


def extended(value, sides, width):
    edges = {}
    for axis, dim in sides:
        devices, length = (lax.axis_size(axis), value.shape[dim])
        up = [(i, (i + 1) % devices) for i in range(devices - 1)]
        last = lax.slice_in_dim(value, length - width, length, axis=dim)
        first = lax.slice_in_dim(value, 0, width, axis=dim)
        edges[dim] = (
            lax.ppermute(last, axis, up),
            lax.ppermute(first, axis, [(b, a) for a, b in up]),
        )
    done = []
    for _, dim in sides:
        low, high = edges[dim]
        around = [(width, width) if d in done else (0, 0) for d in range(value.ndim)]
        value = jnp.concatenate([jnp.pad(low, around), value, jnp.pad(high, around)], axis=dim)
        done.append(dim)
    return value


def partner(block, axis, stride):
    count = lax.axis_size(axis)
    route = []
    for low in range(count):
        high = low | 1 << stride
        if high != low and high < count:
            route += [(low, high), (high, low)]
    return lax.ppermute(block, axis, route)


STAGES = ("dev_0", "sec_0", "sec_1", "dev_1", "dev_2")


def staged_gather(block, fillers):
    value = block
    done = []
    for stage, axis in enumerate(STAGES):
        count = lax.axis_size(axis)
        pieces = [value]
        for shift in range(1, count):
            route = [(i, (i + shift) % count) for i in range(count)]
            pieces.append(lax.ppermute(value, axis, route))
        done.append(fillers[stage]())
        value = jnp.stack(pieces)
    return value.reshape((-1,) + block.shape), done


def slot_of(boxes):
    coords = {}
    rest = boxes
    for axis in reversed(SEC_DEV):
        count = lax.axis_size(axis)
        coords[axis] = rest % count
        rest = rest // count
    slot = jnp.zeros_like(boxes)
    for axis in reversed(STAGES):
        count = lax.axis_size(axis)
        shift = (lax.axis_index(axis) - coords[axis]) % count
        slot = slot * count + shift
    return slot


TWO_OVER_PI = 0.6366197723675814
PIO2_1 = 1.5703125
PIO2_2 = 4.837512969970703125e-4
PIO2_3 = 7.54978995489188216e-8


def sincos(x):
    turns = jnp.round(x * TWO_OVER_PI)
    r = ((x - turns * PIO2_1) - turns * PIO2_2) - turns * PIO2_3
    z = r * r
    s = r + r * z * (-1.6666654611e-1 + z * (8.3321608736e-3 + z * -1.9515295891e-4))
    c = 1.0 - 0.5 * z + z * z * (
        4.166664568298827e-2 + z * (-1.388731625493765e-3 + z * 2.443315711809948e-5)
    )
    quadrant = turns.astype(jnp.int32) & 3
    swap = (quadrant & 1) == 1
    sin_v = jnp.where(swap, c, s)
    cos_v = jnp.where(swap, s, c)
    sin_v = jnp.where(quadrant >= 2, -sin_v, sin_v)
    cos_v = jnp.where((quadrant == 1) | (quadrant == 2), -cos_v, cos_v)
    return sin_v, cos_v


def _apply_body(scale, waves_ref, tgt_ref, src_ref, val_ref, out_ref):
    targets = tgt_ref[0]
    sources = src_ref[0]
    squared = None
    for axis in range(3):
        offset = targets[:, axis : axis + 1] - sources[axis : axis + 1, :]
        squared = offset * offset if squared is None else squared + offset * offset
    distance = jnp.sqrt(squared + SOFT * SOFT)
    amplitude = scale / distance
    dims = (((1,), (1,)), ((), ()))
    highest = lax.Precision.HIGHEST
    for f in range(out_ref.shape[1]):
        phase = waves_ref[f] * distance
        sin_v, cos_v = sincos(phase)
        real_kernel = amplitude * cos_v
        imag_kernel = amplitude * sin_v
        values = val_ref[0, f]
        real_part = lax.dot_general(values, real_kernel, dims, precision=highest, preferred_element_type=jnp.float32)
        imag_part = lax.dot_general(values, imag_kernel, dims, precision=highest, preferred_element_type=jnp.float32)
        out_ref[0, f, 0:1, :] = real_part[0:1] - imag_part[1:2]
        out_ref[0, f, 1:2, :] = real_part[1:2] + imag_part[0:1]


def apply_kernel(targets, sources, values, waves, scale):
    n, a, _ = targets.shape
    b = sources.shape[2]
    f = values.shape[1]
    return pl.pallas_call(
        functools.partial(_apply_body, scale),
        grid=(n,),
        in_specs=[
            pl.BlockSpec(memory_space=pltpu.SMEM),
            pl.BlockSpec((1, a, 3), lambda i: (i, 0, 0)),
            pl.BlockSpec((1, 3, b), lambda i: (i, 0, 0)),
            pl.BlockSpec((1, f, 2, b), lambda i: (i, 0, 0, 0)),
        ],
        out_specs=pl.BlockSpec((1, f, 2, a), lambda i: (i, 0, 0, 0)),
        out_shape=jax.ShapeDtypeStruct((n, f, 2, a), jnp.float32),
    )(waves, targets, sources, values)


def helmholtz(targets, sources, values, waves, scale):
    out = apply_kernel(
        jnp.swapaxes(targets, 1, 2), sources, jnp.swapaxes(values, 1, 2), waves, scale
    )
    return jnp.swapaxes(out, 1, 2)


def staged_sum(value):
    for axis in STAGES:
        count = lax.axis_size(axis)
        position = lax.axis_index(axis)
        for bit in range(count.bit_length() - 1):
            other = partner(value, axis, bit)
            upper = (position >> bit) & 1
            value = jnp.where(upper == 1, other + value, value + other)
    return value


def device_body(
    sources,
    positions,
    weights,
    wavenumbers,
    directions,
    box_centers,
    group_centers,
    near_pairs,
    pair_counts,
    box_lists,
    group_lists,
):
    radius_box = 1.0 + 0.5 * LEAVES
    radius_group = 2.0 * radius_box
    device_index = lax.axis_index(SEC_DEV)
    weighted = sources * weights[None, None, :]
    packed = jnp.concatenate([weighted.reshape(2 * F, P_DEV), positions], axis=0)
    window = extended(packed, ((SEC_DEV, 1),), P_DEV)
    window_values = window[: 2 * F].reshape(2, F, 3 * LEAVES, LEAF)
    window_xyz = window[2 * F :].reshape(3, 3 * LEAVES, LEAF)
    local_xyz = positions.reshape(3, LEAVES, LEAF)
    targets = near_pairs[0, 0]
    anchors = near_pairs[0, 1]
    live_count = pair_counts[0]
    pair_ids = jnp.arange(PAIRS_MAX, dtype=jnp.int32)
    leaf_ids = jnp.arange(LEAVES, dtype=jnp.int32)
    live = (pair_ids < live_count).astype(jnp.float32)
    near_values = jnp.transpose(window_values[:, :, anchors], (2, 0, 1, 3)) * live[:, None, None, None]
    near_targets = jnp.transpose(local_xyz[:, targets], (1, 0, 2))
    near_sources = jnp.transpose(window_xyz[:, anchors], (1, 0, 2))
    chunk = -(-PAIRS_MAX // len(STAGES))

    def near_part(first):
        def run():
            picked = slice(first, min(first + chunk, PAIRS_MAX))
            return helmholtz(
                near_targets[picked], near_sources[picked], near_values[picked], wavenumbers, 1.0
            )

        return run

    fillers = [near_part(k * chunk) for k in range(len(STAGES))]
    own_center = lax.dynamic_index_in_dim(box_centers, device_index, 1, keepdims=False)
    own_proxies = own_center[:, None] + radius_box * directions
    own_multipole = helmholtz(
        own_proxies[None], positions[None], weighted[None], wavenumbers, radius_box
    )[0] / math.sqrt(P_DEV)
    parent = device_index // GROUP
    parent_proxies = (
        lax.dynamic_index_in_dim(group_centers, parent, 1, keepdims=False)[:, None]
        + radius_group * directions
    )
    source_groups = lax.dynamic_index_in_dim(group_lists, parent, 0, keepdims=False)
    contribution = helmholtz(
        parent_proxies[None], own_proxies[None], own_multipole[None], wavenumbers, radius_group
    )[0] / math.sqrt(GROUP * Q)
    group_term = contribution
    for level_bit in range(GROUP.bit_length() - 1):
        group_term = group_term + partner(group_term, DEV, level_bit)
    share_width = Q // GROUP
    member_rank = device_index % GROUP
    share_piece = lax.dynamic_slice_in_dim(group_term, member_rank * share_width, share_width, 2)
    staged, parts = staged_gather(jnp.concatenate([own_multipole, share_piece], axis=2), fillers)
    blocks = jnp.concatenate(parts, axis=0)
    placing = (targets[:, None] == leaf_ids[None, :]).astype(jnp.float32)
    near_total = jnp.einsum(
        "srfa,sl->rfla", blocks, placing, precision=lax.Precision.HIGHEST
    ).reshape(2, F, P_DEV)
    source_boxes = box_lists[0]
    children = source_groups[:, None] * GROUP + jnp.arange(GROUP, dtype=jnp.int32)[None, :]
    source_multipoles = (
        staged[slot_of(children)][..., Q:]
        .transpose(0, 2, 3, 1, 4)
        .reshape(source_groups.shape[0], 2, F, Q)
    )
    source_proxies = box_centers[:, source_boxes][:, :, None] + radius_box * directions[:, None, :]
    incoming = helmholtz(
        jnp.broadcast_to(own_proxies, (source_boxes.shape[0],) + own_proxies.shape),
        jnp.transpose(source_proxies, (1, 0, 2)),
        staged[slot_of(source_boxes)][..., :Q],
        wavenumbers,
        radius_box,
    ).sum(0) / math.sqrt(ML1 * Q)
    group_proxies = (
        group_centers[:, source_groups][:, :, None] + radius_group * directions[:, None, :]
    )
    group_local = helmholtz(
        jnp.broadcast_to(parent_proxies, (source_groups.shape[0],) + parent_proxies.shape),
        jnp.transpose(group_proxies, (1, 0, 2)),
        source_multipoles,
        wavenumbers,
        radius_group,
    ).sum(0) / math.sqrt(ML2 * Q)
    descended = helmholtz(
        own_proxies[None], parent_proxies[None], group_local[None], wavenumbers, radius_group
    )[0] / math.sqrt(Q)
    box_local = incoming + descended
    far_field = helmholtz(
        positions[None], own_proxies[None], box_local[None], wavenumbers, radius_box
    )[0] / math.sqrt(Q)
    result = 0.5 * sources + near_total / math.sqrt(LEAF * PAIRS_LEAF) + far_field
    real_sum = jnp.sum(sources[0] * result[0] + sources[1] * result[1], axis=-1)
    imag_sum = jnp.sum(sources[0] * result[1] - sources[1] * result[0], axis=-1)
    squares = jnp.sum(sources[0] * sources[0] + sources[1] * sources[1], axis=-1)
    sums = staged_sum(jnp.stack([real_sum, imag_sum, squares]))
    rayleigh = sums[:2] / (sums[2] + 1e-06)[None, :]
    return (result, rayleigh)


def solution(mesh):
    split = Mesh(mesh.devices.reshape(2, 4, 4, 4, 2), ("sec_0", "sec_1", "dev_0", "dev_1", "dev_2"))
    placed = (
        P(None, None, SEC_DEV),
        P(None, SEC_DEV),
        P(SEC_DEV),
        P(),
        P(),
        P(),
        P(),
        P(SEC_DEV, None, None),
        P(SEC_DEV),
        P(SEC_DEV, None),
        P(),
    )
    return jax.shard_map(
        device_body,
        mesh=split,
        in_specs=placed,
        out_specs=(P(None, None, SEC_DEV), P()),
        check_vma=False,
    )
```

```python
import functools
import math

import jax
import jax.numpy as jnp
from jax import lax
from jax.experimental import pallas as pl
from jax.experimental.pallas import tpu as pltpu
from jax.sharding import Mesh
from jax.sharding import PartitionSpec as P

LEAF = 128
LEAVES = 2
F = 8
Q = 128
PAIRS_LEAF = 5
ML1 = 4
ML2 = 2
GROUP = 8
P_DEV = 256
PAIRS_MAX = 10
SEC_DEV = ("sec_0", "sec_1", "dev_0", "dev_1", "dev_2")
DEV = ("dev_0", "dev_1", "dev_2")


SOFT = 0.1


def extended(value, sides, width):
    edges = {}
    for axis, dim in sides:
        devices, length = (lax.axis_size(axis), value.shape[dim])
        up = [(i, (i + 1) % devices) for i in range(devices - 1)]
        last = lax.slice_in_dim(value, length - width, length, axis=dim)
        first = lax.slice_in_dim(value, 0, width, axis=dim)
        edges[dim] = (
            lax.ppermute(last, axis, up),
            lax.ppermute(first, axis, [(b, a) for a, b in up]),
        )
    done = []
    for _, dim in sides:
        low, high = edges[dim]
        around = [(width, width) if d in done else (0, 0) for d in range(value.ndim)]
        value = jnp.concatenate([jnp.pad(low, around), value, jnp.pad(high, around)], axis=dim)
        done.append(dim)
    return value


def partner(block, axis, stride):
    count = lax.axis_size(axis)
    route = []
    for low in range(count):
        high = low | 1 << stride
        if high != low and high < count:
            route += [(low, high), (high, low)]
    return lax.ppermute(block, axis, route)


STAGES = ("dev_0", "sec_0", "sec_1", "dev_1", "dev_2")


def staged_gather(block, fillers):
    value = block
    done = []
    for stage, axis in enumerate(STAGES):
        count = lax.axis_size(axis)
        pieces = [value]
        for shift in range(1, count):
            route = [(i, (i + shift) % count) for i in range(count)]
            pieces.append(lax.ppermute(value, axis, route))
        done.append(fillers[stage]())
        value = jnp.stack(pieces)
    return value.reshape((-1,) + block.shape), done


def slot_of(boxes):
    coords = {}
    rest = boxes
    for axis in reversed(SEC_DEV):
        count = lax.axis_size(axis)
        coords[axis] = rest % count
        rest = rest // count
    slot = jnp.zeros_like(boxes)
    for axis in reversed(STAGES):
        count = lax.axis_size(axis)
        shift = (lax.axis_index(axis) - coords[axis]) % count
        slot = slot * count + shift
    return slot


TWO_OVER_PI = 0.6366197723675814
PIO2_1 = 1.5703125
PIO2_2 = 4.837512969970703125e-4
PIO2_3 = 7.54978995489188216e-8


def sincos(x):
    turns = jnp.round(x * TWO_OVER_PI)
    r = ((x - turns * PIO2_1) - turns * PIO2_2) - turns * PIO2_3
    z = r * r
    s = r + r * z * (-1.6666654611e-1 + z * (8.3321608736e-3 + z * -1.9515295891e-4))
    c = 1.0 - 0.5 * z + z * z * (
        4.166664568298827e-2 + z * (-1.388731625493765e-3 + z * 2.443315711809948e-5)
    )
    quadrant = turns.astype(jnp.int32) & 3
    swap = (quadrant & 1) == 1
    sin_v = jnp.where(swap, c, s)
    cos_v = jnp.where(swap, s, c)
    sin_v = jnp.where(quadrant >= 2, -sin_v, sin_v)
    cos_v = jnp.where((quadrant == 1) | (quadrant == 2), -cos_v, cos_v)
    return sin_v, cos_v


def _apply_body(scale, waves_ref, tgt_ref, src_ref, val_ref, out_ref):
    targets = tgt_ref[0]
    sources = src_ref[0]
    squared = None
    for axis in range(3):
        offset = targets[:, axis : axis + 1] - sources[axis : axis + 1, :]
        squared = offset * offset if squared is None else squared + offset * offset
    distance = jnp.sqrt(squared + SOFT * SOFT)
    amplitude = scale / distance
    dims = (((1,), (1,)), ((), ()))
    highest = lax.Precision.HIGHEST
    for f in range(out_ref.shape[1]):
        phase = waves_ref[f] * distance
        sin_v, cos_v = sincos(phase)
        real_kernel = amplitude * cos_v
        imag_kernel = amplitude * sin_v
        values = val_ref[0, f]
        real_part = lax.dot_general(values, real_kernel, dims, precision=highest, preferred_element_type=jnp.float32)
        imag_part = lax.dot_general(values, imag_kernel, dims, precision=highest, preferred_element_type=jnp.float32)
        out_ref[0, f, 0:1, :] = real_part[0:1] - imag_part[1:2]
        out_ref[0, f, 1:2, :] = real_part[1:2] + imag_part[0:1]


def apply_kernel(targets, sources, values, waves, scale):
    n, a, _ = targets.shape
    b = sources.shape[2]
    f = values.shape[1]
    source_block = (lambda i: (i, 0, 0)) if sources.shape[0] == n else (lambda i: (0, 0, 0))
    value_block = (lambda i: (i, 0, 0, 0)) if values.shape[0] == n else (lambda i: (0, 0, 0, 0))
    return pl.pallas_call(
        functools.partial(_apply_body, scale),
        grid=(n,),
        in_specs=[
            pl.BlockSpec(memory_space=pltpu.SMEM),
            pl.BlockSpec((1, a, 3), lambda i: (i, 0, 0)),
            pl.BlockSpec((1, 3, b), source_block),
            pl.BlockSpec((1, f, 2, b), value_block),
        ],
        out_specs=pl.BlockSpec((1, f, 2, a), lambda i: (i, 0, 0, 0)),
        out_shape=jax.ShapeDtypeStruct((n, f, 2, a), jnp.float32),
    )(waves, targets, sources, values)


def helmholtz(targets, sources, values, waves, scale):
    out = apply_kernel(
        jnp.swapaxes(targets, 1, 2), sources, jnp.swapaxes(values, 1, 2), waves, scale
    )
    return jnp.swapaxes(out, 1, 2)


def staged_sum(value):
    for axis in STAGES:
        count = lax.axis_size(axis)
        pieces = [value]
        for shift in range(1, count):
            route = [(i, (i + shift) % count) for i in range(count)]
            pieces.append(lax.ppermute(value, axis, route))
        stacked = jnp.stack(pieces)
        order = (lax.axis_index(axis) - jnp.arange(count, dtype=jnp.int32)) % count
        ordered = stacked[order]
        value = ordered[0]
        for j in range(1, count):
            value = value + ordered[j]
    return value


def device_body(
    sources,
    positions,
    weights,
    wavenumbers,
    directions,
    box_centers,
    group_centers,
    near_pairs,
    pair_counts,
    box_lists,
    group_lists,
):
    radius_box = 1.0 + 0.5 * LEAVES
    radius_group = 2.0 * radius_box
    device_index = lax.axis_index(SEC_DEV)
    weighted = sources * weights[None, None, :]
    packed = jnp.concatenate([weighted.reshape(2 * F, P_DEV), positions], axis=0)
    window = extended(packed, ((SEC_DEV, 1),), P_DEV)
    window_values = window[: 2 * F].reshape(2, F, 3 * LEAVES, LEAF)
    window_xyz = window[2 * F :].reshape(3, 3 * LEAVES, LEAF)
    local_xyz = positions.reshape(3, LEAVES, LEAF)
    targets = near_pairs[0, 0]
    anchors = near_pairs[0, 1]
    live_count = pair_counts[0]
    pair_ids = jnp.arange(PAIRS_MAX, dtype=jnp.int32)
    leaf_ids = jnp.arange(LEAVES, dtype=jnp.int32)
    live = (pair_ids < live_count).astype(jnp.float32)
    near_values = jnp.transpose(window_values[:, :, anchors], (2, 0, 1, 3)) * live[:, None, None, None]
    near_targets = jnp.transpose(local_xyz[:, targets], (1, 0, 2))
    near_sources = jnp.transpose(window_xyz[:, anchors], (1, 0, 2))
    chunk = -(-PAIRS_MAX // len(STAGES))

    def near_part(index):
        def run():
            targets_t, sources_s, values_k = adjoint["prep"]["near"][index]
            return jnp.swapaxes(
                apply_kernel(targets_t, sources_s, values_k, wavenumbers, 1.0), 1, 2
            )

        return run

    near_chunks = []
    for k in range(len(STAGES)):
        picked = slice(k * chunk, min((k + 1) * chunk, PAIRS_MAX))
        near_chunks.append(
            (
                jnp.swapaxes(near_targets[picked], 1, 2),
                near_sources[picked],
                jnp.swapaxes(near_values[picked], 1, 2),
            )
        )
    near_fillers = [near_part(k) for k in range(len(STAGES))]
    adjoint = {}

    def stage_two():
        prep = adjoint["prep"]
        adjoint["own"] = apply_kernel(
            prep["own_t"], prep["positions"], prep["conj"], wavenumbers, radius_box
        )
        adjoint["parent"] = apply_kernel(
            prep["parent_t"], prep["own_s"], adjoint["own"], wavenumbers, radius_group
        )
        return near_fillers[2]()

    def stage_three():
        prep = adjoint["prep"]
        adjoint["boxes"] = apply_kernel(
            prep["boxes_t"], prep["own_s"], adjoint["own"], wavenumbers, radius_box
        )
        adjoint["groups"] = apply_kernel(
            prep["groups_t"], prep["parent_s"], adjoint["parent"], wavenumbers, radius_group
        )
        return near_fillers[3]()

    fillers = list(near_fillers)
    fillers[2] = stage_two
    fillers[3] = stage_three
    own_center = lax.dynamic_index_in_dim(box_centers, device_index, 1, keepdims=False)
    own_proxies = own_center[:, None] + radius_box * directions
    own_multipole = helmholtz(
        own_proxies[None], positions[None], weighted[None], wavenumbers, radius_box
    )[0] / math.sqrt(P_DEV)
    parent = device_index // GROUP
    parent_proxies = (
        lax.dynamic_index_in_dim(group_centers, parent, 1, keepdims=False)[:, None]
        + radius_group * directions
    )
    source_groups = lax.dynamic_index_in_dim(group_lists, parent, 0, keepdims=False)
    contribution = helmholtz(
        parent_proxies[None], own_proxies[None], own_multipole[None], wavenumbers, radius_group
    )[0] / math.sqrt(GROUP * Q)
    group_term = contribution
    for level_bit in range(GROUP.bit_length() - 1):
        group_term = group_term + partner(group_term, DEV, level_bit)
    share_width = Q // GROUP
    member_rank = device_index % GROUP
    share_piece = lax.dynamic_slice_in_dim(group_term, member_rank * share_width, share_width, 2)
    source_boxes = box_lists[0]
    source_proxies = box_centers[:, source_boxes][:, :, None] + radius_box * directions[:, None, :]
    group_proxies = (
        group_centers[:, source_groups][:, :, None] + radius_group * directions[:, None, :]
    )
    prep = {
        "own_t": jnp.swapaxes(own_proxies, 0, 1)[None],
        "positions": positions[None],
        "conj": jnp.stack([sources[0], -sources[1]], axis=1)[None],
        "parent_t": jnp.swapaxes(parent_proxies, 0, 1)[None],
        "own_s": own_proxies[None],
        "parent_s": parent_proxies[None],
        "boxes_t": jnp.transpose(source_proxies, (1, 2, 0)),
        "groups_t": jnp.transpose(group_proxies, (1, 2, 0)),
        "near": near_chunks,
    }
    block, adjoint["prep"] = lax.optimization_barrier(
        (jnp.concatenate([own_multipole, share_piece], axis=2), prep)
    )
    staged, parts = staged_gather(block, fillers)
    blocks = jnp.concatenate(parts, axis=0)
    placing = (targets[:, None] == leaf_ids[None, :]).astype(jnp.float32)
    near_total = jnp.einsum(
        "srfa,sl->rfla", blocks, placing, precision=lax.Precision.HIGHEST
    ).reshape(2, F, P_DEV)
    gathered, shares = staged[..., :Q], staged[..., Q:]
    source_boxes = box_lists[0]
    children = source_groups[:, None] * GROUP + jnp.arange(GROUP, dtype=jnp.int32)[None, :]
    source_multipoles = (
        shares[slot_of(children)]
        .transpose(0, 2, 3, 1, 4)
        .reshape(source_groups.shape[0], 2, F, Q)
    )
    box_multipoles = gathered[slot_of(source_boxes)]

    def complex_dot(left, right):
        real = jnp.sum(left[:, 0] * right[:, 0] - left[:, 1] * right[:, 1], axis=(0, 2))
        imag = jnp.sum(left[:, 0] * right[:, 1] + left[:, 1] * right[:, 0], axis=(0, 2))
        return jnp.stack([real, imag])

    far_quotient = (
        complex_dot(jnp.swapaxes(adjoint["boxes"], 1, 2), box_multipoles) / math.sqrt(ML1 * Q)
        + complex_dot(jnp.swapaxes(adjoint["groups"], 1, 2), source_multipoles)
        / (math.sqrt(ML2 * Q) * math.sqrt(Q))
    ) / math.sqrt(Q)
    early = 0.5 * sources + near_total / math.sqrt(LEAF * PAIRS_LEAF)
    early_real = jnp.sum(sources[0] * early[0] + sources[1] * early[1], axis=-1)
    early_imag = jnp.sum(sources[0] * early[1] - sources[1] * early[0], axis=-1)
    squares = jnp.sum(sources[0] * sources[0] + sources[1] * sources[1], axis=-1)
    partial, early = lax.optimization_barrier(
        (jnp.stack([early_real + far_quotient[0], early_imag + far_quotient[1], squares]), early)
    )
    sums = staged_sum(partial)
    rayleigh = sums[:2] / (sums[2] + 1e-06)[None, :]
    group_local = helmholtz(
        jnp.broadcast_to(parent_proxies, (source_groups.shape[0],) + parent_proxies.shape),
        jnp.transpose(group_proxies, (1, 0, 2)),
        source_multipoles,
        wavenumbers,
        radius_group,
    ).sum(0) / math.sqrt(ML2 * Q)
    incoming = helmholtz(
        jnp.broadcast_to(own_proxies, (source_boxes.shape[0],) + own_proxies.shape),
        jnp.transpose(source_proxies, (1, 0, 2)),
        box_multipoles,
        wavenumbers,
        radius_box,
    ).sum(0) / math.sqrt(ML1 * Q)
    descended = helmholtz(
        own_proxies[None], parent_proxies[None], group_local[None], wavenumbers, radius_group
    )[0] / math.sqrt(Q)
    box_local = incoming + descended
    far_field = helmholtz(
        positions[None], own_proxies[None], box_local[None], wavenumbers, radius_box
    )[0] / math.sqrt(Q)
    result = early + far_field
    return (result, rayleigh)


def solution(mesh):
    split = Mesh(mesh.devices.reshape(2, 4, 4, 4, 2), ("sec_0", "sec_1", "dev_0", "dev_1", "dev_2"))
    placed = (
        P(None, None, SEC_DEV),
        P(None, SEC_DEV),
        P(SEC_DEV),
        P(),
        P(),
        P(),
        P(),
        P(SEC_DEV, None, None),
        P(SEC_DEV),
        P(SEC_DEV, None),
        P(),
    )
    return jax.shard_map(
        device_body,
        mesh=split,
        in_specs=placed,
        out_specs=(P(None, None, SEC_DEV), P()),
        check_vma=False,
    )
```

```python
import functools
import math

import jax
import jax.numpy as jnp
from jax import lax
from jax.experimental import pallas as pl
from jax.experimental.pallas import tpu as pltpu
from jax.sharding import Mesh
from jax.sharding import PartitionSpec as P

LEAF = 128
LEAVES = 2
F = 8
Q = 128
PAIRS_LEAF = 5
ML1 = 4
ML2 = 2
GROUP = 8
P_DEV = 256
PAIRS_MAX = 10
SEC_DEV = ("sec_0", "sec_1", "dev_0", "dev_1", "dev_2")
DEV = ("dev_0", "dev_1", "dev_2")


SOFT = 0.1


def extended(value, sides, width):
    edges = {}
    for axis, dim in sides:
        devices, length = (lax.axis_size(axis), value.shape[dim])
        up = [(i, (i + 1) % devices) for i in range(devices - 1)]
        last = lax.slice_in_dim(value, length - width, length, axis=dim)
        first = lax.slice_in_dim(value, 0, width, axis=dim)
        edges[dim] = (
            lax.ppermute(last, axis, up),
            lax.ppermute(first, axis, [(b, a) for a, b in up]),
        )
    done = []
    for _, dim in sides:
        low, high = edges[dim]
        around = [(width, width) if d in done else (0, 0) for d in range(value.ndim)]
        value = jnp.concatenate([jnp.pad(low, around), value, jnp.pad(high, around)], axis=dim)
        done.append(dim)
    return value


def partner(block, axis, stride):
    count = lax.axis_size(axis)
    route = []
    for low in range(count):
        high = low | 1 << stride
        if high != low and high < count:
            route += [(low, high), (high, low)]
    return lax.ppermute(block, axis, route)


STAGES = ("dev_0", "sec_0", "sec_1", "dev_1", "dev_2")


def staged_gather(block, fillers):
    value = block
    done = []
    for stage, axis in enumerate(STAGES):
        count = lax.axis_size(axis)
        pieces = [value]
        for shift in range(1, count):
            route = [(i, (i + shift) % count) for i in range(count)]
            pieces.append(lax.ppermute(value, axis, route))
        done.append(fillers[stage]())
        if stage + 1 < len(STAGES):
            value = jnp.stack(pieces)
    return [piece.reshape((-1,) + block.shape) for piece in pieces], done


def pick(pieces, slots):
    rows = pieces[0].shape[0]
    chosen = pieces[0][slots % rows]
    for index in range(1, len(pieces)):
        chosen = jnp.where(
            (slots // rows == index)[(...,) + (None,) * (pieces[0].ndim - 1)],
            pieces[index][slots % rows],
            chosen,
        )
    return chosen


def slot_of(boxes):
    coords = {}
    rest = boxes
    for axis in reversed(SEC_DEV):
        count = lax.axis_size(axis)
        coords[axis] = rest % count
        rest = rest // count
    slot = jnp.zeros_like(boxes)
    for axis in reversed(STAGES):
        count = lax.axis_size(axis)
        shift = (lax.axis_index(axis) - coords[axis]) % count
        slot = slot * count + shift
    return slot


TWO_OVER_PI = 0.6366197723675814
PIO2_1 = 1.5703125
PIO2_2 = 4.837512969970703125e-4
PIO2_3 = 7.54978995489188216e-8


def sincos(x):
    turns = jnp.round(x * TWO_OVER_PI)
    r = ((x - turns * PIO2_1) - turns * PIO2_2) - turns * PIO2_3
    z = r * r
    s = r + r * z * (-1.6666654611e-1 + z * (8.3321608736e-3 + z * -1.9515295891e-4))
    c = 1.0 - 0.5 * z + z * z * (
        4.166664568298827e-2 + z * (-1.388731625493765e-3 + z * 2.443315711809948e-5)
    )
    quadrant = turns.astype(jnp.int32) & 3
    swap = (quadrant & 1) == 1
    sin_v = jnp.where(swap, c, s)
    cos_v = jnp.where(swap, s, c)
    sin_v = jnp.where(quadrant >= 2, -sin_v, sin_v)
    cos_v = jnp.where((quadrant == 1) | (quadrant == 2), -cos_v, cos_v)
    return sin_v, cos_v


def _apply_body(scale, waves_ref, tgt_ref, src_ref, val_ref, out_ref):
    targets = tgt_ref[0]
    sources = src_ref[0]
    squared = None
    for axis in range(3):
        offset = targets[:, axis : axis + 1] - sources[axis : axis + 1, :]
        squared = offset * offset if squared is None else squared + offset * offset
    distance = jnp.sqrt(squared + SOFT * SOFT)
    amplitude = scale / distance
    dims = (((1,), (1,)), ((), ()))
    highest = lax.Precision.HIGHEST
    for f in range(out_ref.shape[1]):
        phase = waves_ref[f] * distance
        sin_v, cos_v = sincos(phase)
        real_kernel = amplitude * cos_v
        imag_kernel = amplitude * sin_v
        values = val_ref[0, f]
        real_part = lax.dot_general(values, real_kernel, dims, precision=highest, preferred_element_type=jnp.float32)
        imag_part = lax.dot_general(values, imag_kernel, dims, precision=highest, preferred_element_type=jnp.float32)
        out_ref[0, f, 0:1, :] = real_part[0:1] - imag_part[1:2]
        out_ref[0, f, 1:2, :] = real_part[1:2] + imag_part[0:1]


def apply_kernel(targets, sources, values, waves, scale):
    n, a, _ = targets.shape
    b = sources.shape[2]
    f = values.shape[1]
    return pl.pallas_call(
        functools.partial(_apply_body, scale),
        grid=(n,),
        in_specs=[
            pl.BlockSpec(memory_space=pltpu.SMEM),
            pl.BlockSpec((1, a, 3), lambda i: (i, 0, 0)),
            pl.BlockSpec((1, 3, b), lambda i: (i, 0, 0)),
            pl.BlockSpec((1, f, 2, b), lambda i: (i, 0, 0, 0)),
        ],
        out_specs=pl.BlockSpec((1, f, 2, a), lambda i: (i, 0, 0, 0)),
        out_shape=jax.ShapeDtypeStruct((n, f, 2, a), jnp.float32),
    )(waves, targets, sources, values)


def helmholtz(targets, sources, values, waves, scale):
    out = apply_kernel(
        jnp.swapaxes(targets, 1, 2), sources, jnp.swapaxes(values, 1, 2), waves, scale
    )
    return jnp.swapaxes(out, 1, 2)


def staged_sum(value):
    for axis in STAGES:
        count = lax.axis_size(axis)
        pieces = [value]
        for shift in range(1, count):
            route = [(i, (i + shift) % count) for i in range(count)]
            pieces.append(lax.ppermute(value, axis, route))
        stacked = jnp.stack(pieces)
        order = (lax.axis_index(axis) - jnp.arange(count, dtype=jnp.int32)) % count
        ordered = stacked[order]
        value = ordered[0]
        for j in range(1, count):
            value = value + ordered[j]
    return value


def device_body(
    sources,
    positions,
    weights,
    wavenumbers,
    directions,
    box_centers,
    group_centers,
    near_pairs,
    pair_counts,
    box_lists,
    group_lists,
):
    radius_box = 1.0 + 0.5 * LEAVES
    radius_group = 2.0 * radius_box
    device_index = lax.axis_index(SEC_DEV)
    weighted = sources * weights[None, None, :]
    packed = jnp.concatenate([weighted.reshape(2 * F, P_DEV), positions], axis=0)
    window = extended(packed, ((SEC_DEV, 1),), P_DEV)
    window_values = window[: 2 * F].reshape(2, F, 3 * LEAVES, LEAF)
    window_xyz = window[2 * F :].reshape(3, 3 * LEAVES, LEAF)
    local_xyz = positions.reshape(3, LEAVES, LEAF)
    targets = near_pairs[0, 0]
    anchors = near_pairs[0, 1]
    live_count = pair_counts[0]
    pair_ids = jnp.arange(PAIRS_MAX, dtype=jnp.int32)
    leaf_ids = jnp.arange(LEAVES, dtype=jnp.int32)
    live = (pair_ids < live_count).astype(jnp.float32)
    near_values = jnp.transpose(window_values[:, :, anchors], (2, 0, 1, 3)) * live[:, None, None, None]
    near_targets = jnp.transpose(local_xyz[:, targets], (1, 0, 2))
    near_sources = jnp.transpose(window_xyz[:, anchors], (1, 0, 2))
    chunk = -(-PAIRS_MAX // len(STAGES))

    def near_part(first):
        def run():
            picked = slice(first, min(first + chunk, PAIRS_MAX))
            return helmholtz(
                near_targets[picked], near_sources[picked], near_values[picked], wavenumbers, 1.0
            )

        return run

    fillers = [near_part(k * chunk) for k in range(len(STAGES))]
    own_center = lax.dynamic_index_in_dim(box_centers, device_index, 1, keepdims=False)
    own_proxies = own_center[:, None] + radius_box * directions
    own_multipole = helmholtz(
        own_proxies[None], positions[None], weighted[None], wavenumbers, radius_box
    )[0] / math.sqrt(P_DEV)
    parent = device_index // GROUP
    parent_proxies = (
        lax.dynamic_index_in_dim(group_centers, parent, 1, keepdims=False)[:, None]
        + radius_group * directions
    )
    source_groups = lax.dynamic_index_in_dim(group_lists, parent, 0, keepdims=False)
    contribution = helmholtz(
        parent_proxies[None], own_proxies[None], own_multipole[None], wavenumbers, radius_group
    )[0] / math.sqrt(GROUP * Q)
    group_term = contribution
    for level_bit in range(GROUP.bit_length() - 1):
        group_term = group_term + partner(group_term, DEV, level_bit)
    share_width = Q // GROUP
    member_rank = device_index % GROUP
    share_piece = lax.dynamic_slice_in_dim(group_term, member_rank * share_width, share_width, 2)
    staged, parts = staged_gather(jnp.concatenate([own_multipole, share_piece], axis=2), fillers)
    blocks = jnp.concatenate(parts, axis=0)
    placing = (targets[:, None] == leaf_ids[None, :]).astype(jnp.float32)
    near_total = jnp.einsum(
        "srfa,sl->rfla", blocks, placing, precision=lax.Precision.HIGHEST
    ).reshape(2, F, P_DEV)
    source_boxes = box_lists[0]
    children = source_groups[:, None] * GROUP + jnp.arange(GROUP, dtype=jnp.int32)[None, :]
    source_multipoles = (
        pick(staged, slot_of(children))[..., Q:]
        .transpose(0, 2, 3, 1, 4)
        .reshape(source_groups.shape[0], 2, F, Q)
    )
    source_proxies = box_centers[:, source_boxes][:, :, None] + radius_box * directions[:, None, :]
    incoming = helmholtz(
        jnp.broadcast_to(own_proxies, (source_boxes.shape[0],) + own_proxies.shape),
        jnp.transpose(source_proxies, (1, 0, 2)),
        pick(staged, slot_of(source_boxes))[..., :Q],
        wavenumbers,
        radius_box,
    ).sum(0) / math.sqrt(ML1 * Q)
    group_proxies = (
        group_centers[:, source_groups][:, :, None] + radius_group * directions[:, None, :]
    )
    group_local = helmholtz(
        jnp.broadcast_to(parent_proxies, (source_groups.shape[0],) + parent_proxies.shape),
        jnp.transpose(group_proxies, (1, 0, 2)),
        source_multipoles,
        wavenumbers,
        radius_group,
    ).sum(0) / math.sqrt(ML2 * Q)
    descended = helmholtz(
        own_proxies[None], parent_proxies[None], group_local[None], wavenumbers, radius_group
    )[0] / math.sqrt(Q)
    box_local = incoming + descended
    far_field = helmholtz(
        positions[None], own_proxies[None], box_local[None], wavenumbers, radius_box
    )[0] / math.sqrt(Q)
    result = 0.5 * sources + near_total / math.sqrt(LEAF * PAIRS_LEAF) + far_field
    real_sum = jnp.sum(sources[0] * result[0] + sources[1] * result[1], axis=-1)
    imag_sum = jnp.sum(sources[0] * result[1] - sources[1] * result[0], axis=-1)
    squares = jnp.sum(sources[0] * sources[0] + sources[1] * sources[1], axis=-1)
    sums = staged_sum(jnp.stack([real_sum, imag_sum, squares]))
    rayleigh = sums[:2] / (sums[2] + 1e-06)[None, :]
    return (result, rayleigh)


def solution(mesh):
    split = Mesh(mesh.devices.reshape(2, 4, 4, 4, 2), ("sec_0", "sec_1", "dev_0", "dev_1", "dev_2"))
    placed = (
        P(None, None, SEC_DEV),
        P(None, SEC_DEV),
        P(SEC_DEV),
        P(),
        P(),
        P(),
        P(),
        P(SEC_DEV, None, None),
        P(SEC_DEV),
        P(SEC_DEV, None),
        P(),
    )
    return jax.shard_map(
        device_body,
        mesh=split,
        in_specs=placed,
        out_specs=(P(None, None, SEC_DEV), P()),
        check_vma=False,
    )
```

```python
import functools
import math

import jax
import jax.numpy as jnp
from jax import lax
from jax.experimental import pallas as pl
from jax.experimental.pallas import tpu as pltpu
from jax.sharding import Mesh
from jax.sharding import PartitionSpec as P

LEAF = 128
LEAVES = 2
F = 8
Q = 128
PAIRS_LEAF = 5
ML1 = 4
ML2 = 2
GROUP = 8
P_DEV = 256
PAIRS_MAX = 10
SEC_DEV = ("sec_0", "sec_1", "dev_0", "dev_1", "dev_2")


SOFT = 0.1


def extended(value, sides, width):
    edges = {}
    for axis, dim in sides:
        devices, length = (lax.axis_size(axis), value.shape[dim])
        up = [(i, (i + 1) % devices) for i in range(devices - 1)]
        last = lax.slice_in_dim(value, length - width, length, axis=dim)
        first = lax.slice_in_dim(value, 0, width, axis=dim)
        edges[dim] = (
            lax.ppermute(last, axis, up),
            lax.ppermute(first, axis, [(b, a) for a, b in up]),
        )
    done = []
    for _, dim in sides:
        low, high = edges[dim]
        around = [(width, width) if d in done else (0, 0) for d in range(value.ndim)]
        value = jnp.concatenate([jnp.pad(low, around), value, jnp.pad(high, around)], axis=dim)
        done.append(dim)
    return value


STAGES = ("dev_0", "sec_0", "sec_1", "dev_1", "dev_2")


def staged_gather(block, fillers):
    value = block
    done = []
    for stage, axis in enumerate(STAGES):
        count = lax.axis_size(axis)
        pieces = [value]
        for shift in range(1, count):
            route = [(i, (i + shift) % count) for i in range(count)]
            pieces.append(lax.ppermute(value, axis, route))
        done.append(fillers[stage]())
        value = jnp.stack(pieces)
    return value.reshape((-1,) + block.shape), done


def slot_of(boxes):
    coords = {}
    rest = boxes
    for axis in reversed(SEC_DEV):
        count = lax.axis_size(axis)
        coords[axis] = rest % count
        rest = rest // count
    slot = jnp.zeros_like(boxes)
    for axis in reversed(STAGES):
        count = lax.axis_size(axis)
        shift = (lax.axis_index(axis) - coords[axis]) % count
        slot = slot * count + shift
    return slot


TWO_OVER_PI = 0.6366197723675814
PIO2_1 = 1.5703125
PIO2_2 = 4.837512969970703125e-4
PIO2_3 = 7.54978995489188216e-8


def sincos(x):
    turns = jnp.round(x * TWO_OVER_PI)
    r = ((x - turns * PIO2_1) - turns * PIO2_2) - turns * PIO2_3
    z = r * r
    s = r + r * z * (-1.6666654611e-1 + z * (8.3321608736e-3 + z * -1.9515295891e-4))
    c = 1.0 - 0.5 * z + z * z * (
        4.166664568298827e-2 + z * (-1.388731625493765e-3 + z * 2.443315711809948e-5)
    )
    quadrant = turns.astype(jnp.int32) & 3
    swap = (quadrant & 1) == 1
    sin_v = jnp.where(swap, c, s)
    cos_v = jnp.where(swap, s, c)
    sin_v = jnp.where(quadrant >= 2, -sin_v, sin_v)
    cos_v = jnp.where((quadrant == 1) | (quadrant == 2), -cos_v, cos_v)
    return sin_v, cos_v


def _apply_body(scale, waves_ref, tgt_ref, src_ref, val_ref, out_ref):
    targets = tgt_ref[0]
    sources = src_ref[0]
    squared = None
    for axis in range(3):
        offset = targets[:, axis : axis + 1] - sources[axis : axis + 1, :]
        squared = offset * offset if squared is None else squared + offset * offset
    distance = jnp.sqrt(squared + SOFT * SOFT)
    amplitude = scale / distance
    dims = (((1,), (1,)), ((), ()))
    highest = lax.Precision.HIGHEST
    for f in range(out_ref.shape[1]):
        phase = waves_ref[f] * distance
        sin_v, cos_v = sincos(phase)
        real_kernel = amplitude * cos_v
        imag_kernel = amplitude * sin_v
        values = val_ref[0, f]
        real_part = lax.dot_general(values, real_kernel, dims, precision=highest, preferred_element_type=jnp.float32)
        imag_part = lax.dot_general(values, imag_kernel, dims, precision=highest, preferred_element_type=jnp.float32)
        out_ref[0, f, 0:1, :] = real_part[0:1] - imag_part[1:2]
        out_ref[0, f, 1:2, :] = real_part[1:2] + imag_part[0:1]


def apply_kernel(targets, sources, values, waves, scale):
    n, a, _ = targets.shape
    b = sources.shape[2]
    f = values.shape[1]
    return pl.pallas_call(
        functools.partial(_apply_body, scale),
        grid=(n,),
        in_specs=[
            pl.BlockSpec(memory_space=pltpu.SMEM),
            pl.BlockSpec((1, a, 3), lambda i: (i, 0, 0)),
            pl.BlockSpec((1, 3, b), lambda i: (i, 0, 0)),
            pl.BlockSpec((1, f, 2, b), lambda i: (i, 0, 0, 0)),
        ],
        out_specs=pl.BlockSpec((1, f, 2, a), lambda i: (i, 0, 0, 0)),
        out_shape=jax.ShapeDtypeStruct((n, f, 2, a), jnp.float32),
    )(waves, targets, sources, values)


def helmholtz(targets, sources, values, waves, scale):
    out = apply_kernel(
        jnp.swapaxes(targets, 1, 2), sources, jnp.swapaxes(values, 1, 2), waves, scale
    )
    return jnp.swapaxes(out, 1, 2)


def staged_sum(value):
    for axis in STAGES:
        count = lax.axis_size(axis)
        pieces = [value]
        for shift in range(1, count):
            route = [(i, (i + shift) % count) for i in range(count)]
            pieces.append(lax.ppermute(value, axis, route))
        stacked = jnp.stack(pieces)
        order = (lax.axis_index(axis) - jnp.arange(count, dtype=jnp.int32)) % count
        ordered = stacked[order]
        value = ordered[0]
        for j in range(1, count):
            value = value + ordered[j]
    return value


def device_body(
    sources,
    positions,
    weights,
    wavenumbers,
    directions,
    box_centers,
    group_centers,
    near_pairs,
    pair_counts,
    box_lists,
    group_lists,
):
    radius_box = 1.0 + 0.5 * LEAVES
    radius_group = 2.0 * radius_box
    device_index = lax.axis_index(SEC_DEV)
    weighted = sources * weights[None, None, :]
    packed = jnp.concatenate([weighted.reshape(2 * F, P_DEV), positions], axis=0)
    window = extended(packed, ((SEC_DEV, 1),), P_DEV)
    window_values = window[: 2 * F].reshape(2, F, 3 * LEAVES, LEAF)
    window_xyz = window[2 * F :].reshape(3, 3 * LEAVES, LEAF)
    local_xyz = positions.reshape(3, LEAVES, LEAF)
    targets = near_pairs[0, 0]
    anchors = near_pairs[0, 1]
    live_count = pair_counts[0]
    pair_ids = jnp.arange(PAIRS_MAX, dtype=jnp.int32)
    leaf_ids = jnp.arange(LEAVES, dtype=jnp.int32)
    live = (pair_ids < live_count).astype(jnp.float32)
    near_values = jnp.transpose(window_values[:, :, anchors], (2, 0, 1, 3)) * live[:, None, None, None]
    near_targets = jnp.transpose(local_xyz[:, targets], (1, 0, 2))
    near_sources = jnp.transpose(window_xyz[:, anchors], (1, 0, 2))
    chunk = -(-PAIRS_MAX // len(STAGES))

    def near_part(first):
        def run():
            picked = slice(first, min(first + chunk, PAIRS_MAX))
            return helmholtz(
                near_targets[picked], near_sources[picked], near_values[picked], wavenumbers, 1.0
            )

        return run

    fillers = [near_part(k * chunk) for k in range(len(STAGES))]
    own_center = lax.dynamic_index_in_dim(box_centers, device_index, 1, keepdims=False)
    own_proxies = own_center[:, None] + radius_box * directions
    own_multipole = helmholtz(
        own_proxies[None], positions[None], weighted[None], wavenumbers, radius_box
    )[0] / math.sqrt(P_DEV)
    parent = device_index // GROUP
    parent_proxies = (
        lax.dynamic_index_in_dim(group_centers, parent, 1, keepdims=False)[:, None]
        + radius_group * directions
    )
    source_groups = lax.dynamic_index_in_dim(group_lists, parent, 0, keepdims=False)
    contribution = helmholtz(
        parent_proxies[None], own_proxies[None], own_multipole[None], wavenumbers, radius_group
    )[0] / math.sqrt(GROUP * Q)
    staged, parts = staged_gather(jnp.concatenate([own_multipole, contribution], axis=2), fillers)
    blocks = jnp.concatenate(parts, axis=0)
    placing = (targets[:, None] == leaf_ids[None, :]).astype(jnp.float32)
    near_total = jnp.einsum(
        "srfa,sl->rfla", blocks, placing, precision=lax.Precision.HIGHEST
    ).reshape(2, F, P_DEV)
    source_boxes = box_lists[0]
    children = source_groups[:, None] * GROUP + jnp.arange(GROUP, dtype=jnp.int32)[None, :]
    source_multipoles = staged[slot_of(children)][..., Q:].sum(1)
    source_proxies = box_centers[:, source_boxes][:, :, None] + radius_box * directions[:, None, :]
    incoming = helmholtz(
        jnp.broadcast_to(own_proxies, (source_boxes.shape[0],) + own_proxies.shape),
        jnp.transpose(source_proxies, (1, 0, 2)),
        staged[slot_of(source_boxes)][..., :Q],
        wavenumbers,
        radius_box,
    ).sum(0) / math.sqrt(ML1 * Q)
    group_proxies = (
        group_centers[:, source_groups][:, :, None] + radius_group * directions[:, None, :]
    )
    group_local = helmholtz(
        jnp.broadcast_to(parent_proxies, (source_groups.shape[0],) + parent_proxies.shape),
        jnp.transpose(group_proxies, (1, 0, 2)),
        source_multipoles,
        wavenumbers,
        radius_group,
    ).sum(0) / math.sqrt(ML2 * Q)
    descended = helmholtz(
        own_proxies[None], parent_proxies[None], group_local[None], wavenumbers, radius_group
    )[0] / math.sqrt(Q)
    box_local = incoming + descended
    far_field = helmholtz(
        positions[None], own_proxies[None], box_local[None], wavenumbers, radius_box
    )[0] / math.sqrt(Q)
    result = 0.5 * sources + near_total / math.sqrt(LEAF * PAIRS_LEAF) + far_field
    real_sum = jnp.sum(sources[0] * result[0] + sources[1] * result[1], axis=-1)
    imag_sum = jnp.sum(sources[0] * result[1] - sources[1] * result[0], axis=-1)
    squares = jnp.sum(sources[0] * sources[0] + sources[1] * sources[1], axis=-1)
    sums = staged_sum(jnp.stack([real_sum, imag_sum, squares]))
    rayleigh = sums[:2] / (sums[2] + 1e-06)[None, :]
    return (result, rayleigh)


def solution(mesh):
    split = Mesh(mesh.devices.reshape(2, 4, 4, 4, 2), ("sec_0", "sec_1", "dev_0", "dev_1", "dev_2"))
    placed = (
        P(None, None, SEC_DEV),
        P(None, SEC_DEV),
        P(SEC_DEV),
        P(),
        P(),
        P(),
        P(),
        P(SEC_DEV, None, None),
        P(SEC_DEV),
        P(SEC_DEV, None),
        P(),
    )
    return jax.shard_map(
        device_body,
        mesh=split,
        in_specs=placed,
        out_specs=(P(None, None, SEC_DEV), P()),
        check_vma=False,
    )
```

```python
import functools
import math

import jax
import jax.numpy as jnp
from jax import lax
from jax.experimental import pallas as pl
from jax.experimental.pallas import tpu as pltpu
from jax.sharding import Mesh
from jax.sharding import PartitionSpec as P

LEAF = 128
LEAVES = 2
F = 8
Q = 128
PAIRS_LEAF = 5
ML1 = 4
ML2 = 2
GROUP = 8
P_DEV = 256
PAIRS_MAX = 10
SEC_DEV = ("sec_0", "sec_1", "dev_0", "dev_1", "dev_2")


SOFT = 0.1


def extended(value, sides, width):
    edges = {}
    for axis, dim in sides:
        devices, length = (lax.axis_size(axis), value.shape[dim])
        up = [(i, (i + 1) % devices) for i in range(devices - 1)]
        last = lax.slice_in_dim(value, length - width, length, axis=dim)
        first = lax.slice_in_dim(value, 0, width, axis=dim)
        edges[dim] = (
            lax.ppermute(last, axis, up),
            lax.ppermute(first, axis, [(b, a) for a, b in up]),
        )
    done = []
    for _, dim in sides:
        low, high = edges[dim]
        around = [(width, width) if d in done else (0, 0) for d in range(value.ndim)]
        value = jnp.concatenate([jnp.pad(low, around), value, jnp.pad(high, around)], axis=dim)
        done.append(dim)
    return value


STAGES = ("dev_0", "sec_0", "sec_1", "dev_1", "dev_2")


def staged_gather(block, fillers):
    value = block
    done = []
    for stage, axis in enumerate(STAGES):
        count = lax.axis_size(axis)
        pieces = [value]
        for shift in range(1, count):
            route = [(i, (i + shift) % count) for i in range(count)]
            pieces.append(lax.ppermute(value, axis, route))
        done.append(fillers[stage]())
        value = jnp.stack(pieces)
    return value.reshape((-1,) + block.shape), done


def slot_of(boxes):
    coords = {}
    rest = boxes
    for axis in reversed(SEC_DEV):
        count = lax.axis_size(axis)
        coords[axis] = rest % count
        rest = rest // count
    slot = jnp.zeros_like(boxes)
    for axis in reversed(STAGES):
        count = lax.axis_size(axis)
        shift = (lax.axis_index(axis) - coords[axis]) % count
        slot = slot * count + shift
    return slot


TWO_OVER_PI = 0.6366197723675814
PIO2_1 = 1.5703125
PIO2_2 = 4.837512969970703125e-4
PIO2_3 = 7.54978995489188216e-8


def sincos(x):
    turns = jnp.round(x * TWO_OVER_PI)
    r = ((x - turns * PIO2_1) - turns * PIO2_2) - turns * PIO2_3
    z = r * r
    s = r + r * z * (-1.6666654611e-1 + z * (8.3321608736e-3 + z * -1.9515295891e-4))
    c = 1.0 - 0.5 * z + z * z * (
        4.166664568298827e-2 + z * (-1.388731625493765e-3 + z * 2.443315711809948e-5)
    )
    quadrant = turns.astype(jnp.int32) & 3
    swap = (quadrant & 1) == 1
    sin_v = jnp.where(swap, c, s)
    cos_v = jnp.where(swap, s, c)
    sin_v = jnp.where(quadrant >= 2, -sin_v, sin_v)
    cos_v = jnp.where((quadrant == 1) | (quadrant == 2), -cos_v, cos_v)
    return sin_v, cos_v


def _apply_body(scale, waves_ref, tgt_ref, src_ref, val_ref, out_ref):
    targets = tgt_ref[0]
    sources = src_ref[0]
    squared = None
    for axis in range(3):
        offset = targets[:, axis : axis + 1] - sources[axis : axis + 1, :]
        squared = offset * offset if squared is None else squared + offset * offset
    distance = jnp.sqrt(squared + SOFT * SOFT)
    amplitude = scale / distance
    dims = (((1,), (1,)), ((), ()))
    highest = lax.Precision.HIGHEST
    for f in range(out_ref.shape[1]):
        phase = waves_ref[f] * distance
        sin_v, cos_v = sincos(phase)
        real_kernel = amplitude * cos_v
        imag_kernel = amplitude * sin_v
        values = val_ref[0, f]
        real_part = lax.dot_general(values, real_kernel, dims, precision=highest, preferred_element_type=jnp.float32)
        imag_part = lax.dot_general(values, imag_kernel, dims, precision=highest, preferred_element_type=jnp.float32)
        out_ref[0, f, 0:1, :] = real_part[0:1] - imag_part[1:2]
        out_ref[0, f, 1:2, :] = real_part[1:2] + imag_part[0:1]


def apply_kernel(targets, sources, values, waves, scale):
    n, a, _ = targets.shape
    b = sources.shape[2]
    f = values.shape[1]
    return pl.pallas_call(
        functools.partial(_apply_body, scale),
        grid=(n,),
        in_specs=[
            pl.BlockSpec(memory_space=pltpu.SMEM),
            pl.BlockSpec((1, a, 3), lambda i: (i, 0, 0)),
            pl.BlockSpec((1, 3, b), lambda i: (i, 0, 0)),
            pl.BlockSpec((1, f, 2, b), lambda i: (i, 0, 0, 0)),
        ],
        out_specs=pl.BlockSpec((1, f, 2, a), lambda i: (i, 0, 0, 0)),
        out_shape=jax.ShapeDtypeStruct((n, f, 2, a), jnp.float32),
    )(waves, targets, sources, values)


def helmholtz(targets, sources, values, waves, scale):
    out = apply_kernel(
        jnp.swapaxes(targets, 1, 2), sources, jnp.swapaxes(values, 1, 2), waves, scale
    )
    return jnp.swapaxes(out, 1, 2)


def staged_sum(value):
    for axis in STAGES:
        count = lax.axis_size(axis)
        pieces = [value]
        for shift in range(1, count):
            route = [(i, (i + shift) % count) for i in range(count)]
            pieces.append(lax.ppermute(value, axis, route))
        stacked = jnp.stack(pieces)
        order = (lax.axis_index(axis) - jnp.arange(count, dtype=jnp.int32)) % count
        ordered = stacked[order]
        value = ordered[0]
        for j in range(1, count):
            value = value + ordered[j]
    return value


def device_body(
    sources,
    positions,
    weights,
    wavenumbers,
    directions,
    box_centers,
    group_centers,
    near_pairs,
    pair_counts,
    box_lists,
    group_lists,
):
    radius_box = 1.0 + 0.5 * LEAVES
    radius_group = 2.0 * radius_box
    device_index = lax.axis_index(SEC_DEV)
    weighted = sources * weights[None, None, :]
    packed = jnp.concatenate([weighted.reshape(2 * F, P_DEV), positions], axis=0)
    window = extended(packed, ((SEC_DEV, 1),), P_DEV)
    window_values = window[: 2 * F].reshape(2, F, 3 * LEAVES, LEAF)
    window_xyz = window[2 * F :].reshape(3, 3 * LEAVES, LEAF)
    local_xyz = positions.reshape(3, LEAVES, LEAF)
    targets = near_pairs[0, 0]
    anchors = near_pairs[0, 1]
    live_count = pair_counts[0]
    pair_ids = jnp.arange(PAIRS_MAX, dtype=jnp.int32)
    leaf_ids = jnp.arange(LEAVES, dtype=jnp.int32)
    live = (pair_ids < live_count).astype(jnp.float32)
    near_values = jnp.transpose(window_values[:, :, anchors], (2, 0, 1, 3)) * live[:, None, None, None]
    near_targets = jnp.transpose(local_xyz[:, targets], (1, 0, 2))
    near_sources = jnp.transpose(window_xyz[:, anchors], (1, 0, 2))
    chunk = -(-PAIRS_MAX // len(STAGES))

    def near_part(first):
        def run():
            picked = slice(first, min(first + chunk, PAIRS_MAX))
            return helmholtz(
                near_targets[picked], near_sources[picked], near_values[picked], wavenumbers, 1.0
            )

        return run

    near_runs = [near_part(k * chunk) for k in range(len(STAGES))]
    fillers = [lambda: [near_runs[0]()], lambda: [near_runs[1]()], lambda: [near_runs[2]()]]
    fillers += [lambda: [near_runs[3](), near_runs[4]()], lambda: []]
    own_center = lax.dynamic_index_in_dim(box_centers, device_index, 1, keepdims=False)
    own_proxies = own_center[:, None] + radius_box * directions
    own_multipole = helmholtz(
        own_proxies[None], positions[None], weighted[None], wavenumbers, radius_box
    )[0] / math.sqrt(P_DEV)
    parent = device_index // GROUP
    parent_proxies = (
        lax.dynamic_index_in_dim(group_centers, parent, 1, keepdims=False)[:, None]
        + radius_group * directions
    )
    source_groups = lax.dynamic_index_in_dim(group_lists, parent, 0, keepdims=False)
    contribution = helmholtz(
        parent_proxies[None], own_proxies[None], own_multipole[None], wavenumbers, radius_group
    )[0] / math.sqrt(GROUP * Q)
    staged, parts = staged_gather(jnp.concatenate([own_multipole, contribution], axis=2), fillers)
    blocks = jnp.concatenate([block for group in parts for block in group], axis=0)
    placing = (targets[:, None] == leaf_ids[None, :]).astype(jnp.float32)
    near_total = jnp.einsum(
        "srfa,sl->rfla", blocks, placing, precision=lax.Precision.HIGHEST
    ).reshape(2, F, P_DEV)
    source_boxes = box_lists[0]
    children = source_groups[:, None] * GROUP + jnp.arange(GROUP, dtype=jnp.int32)[None, :]
    source_multipoles = staged[slot_of(children)][..., Q:].sum(1)
    source_proxies = box_centers[:, source_boxes][:, :, None] + radius_box * directions[:, None, :]
    incoming = helmholtz(
        jnp.broadcast_to(own_proxies, (source_boxes.shape[0],) + own_proxies.shape),
        jnp.transpose(source_proxies, (1, 0, 2)),
        staged[slot_of(source_boxes)][..., :Q],
        wavenumbers,
        radius_box,
    ).sum(0) / math.sqrt(ML1 * Q)
    group_proxies = (
        group_centers[:, source_groups][:, :, None] + radius_group * directions[:, None, :]
    )
    group_local = helmholtz(
        jnp.broadcast_to(parent_proxies, (source_groups.shape[0],) + parent_proxies.shape),
        jnp.transpose(group_proxies, (1, 0, 2)),
        source_multipoles,
        wavenumbers,
        radius_group,
    ).sum(0) / math.sqrt(ML2 * Q)
    descended = helmholtz(
        own_proxies[None], parent_proxies[None], group_local[None], wavenumbers, radius_group
    )[0] / math.sqrt(Q)
    box_local = incoming + descended
    far_field = helmholtz(
        positions[None], own_proxies[None], box_local[None], wavenumbers, radius_box
    )[0] / math.sqrt(Q)
    result = 0.5 * sources + near_total / math.sqrt(LEAF * PAIRS_LEAF) + far_field
    real_sum = jnp.sum(sources[0] * result[0] + sources[1] * result[1], axis=-1)
    imag_sum = jnp.sum(sources[0] * result[1] - sources[1] * result[0], axis=-1)
    squares = jnp.sum(sources[0] * sources[0] + sources[1] * sources[1], axis=-1)
    sums = staged_sum(jnp.stack([real_sum, imag_sum, squares]))
    rayleigh = sums[:2] / (sums[2] + 1e-06)[None, :]
    return (result, rayleigh)


def solution(mesh):
    split = Mesh(mesh.devices.reshape(2, 4, 4, 4, 2), ("sec_0", "sec_1", "dev_0", "dev_1", "dev_2"))
    placed = (
        P(None, None, SEC_DEV),
        P(None, SEC_DEV),
        P(SEC_DEV),
        P(),
        P(),
        P(),
        P(),
        P(SEC_DEV, None, None),
        P(SEC_DEV),
        P(SEC_DEV, None),
        P(),
    )
    return jax.shard_map(
        device_body,
        mesh=split,
        in_specs=placed,
        out_specs=(P(None, None, SEC_DEV), P()),
        check_vma=False,
    )
```

```python
import functools
import math

import jax
import jax.numpy as jnp
from jax import lax
from jax.experimental import pallas as pl
from jax.experimental.pallas import tpu as pltpu
from jax.sharding import Mesh
from jax.sharding import PartitionSpec as P

LEAF = 128
LEAVES = 2
F = 8
Q = 128
PAIRS_LEAF = 5
ML1 = 4
ML2 = 2
GROUP = 8
P_DEV = 256
PAIRS_MAX = 10
SEC_DEV = ("sec_0", "sec_1", "dev_0", "dev_1", "dev_2")


SOFT = 0.1


def extended(value, sides, width):
    edges = {}
    for axis, dim in sides:
        devices, length = (lax.axis_size(axis), value.shape[dim])
        up = [(i, (i + 1) % devices) for i in range(devices - 1)]
        last = lax.slice_in_dim(value, length - width, length, axis=dim)
        first = lax.slice_in_dim(value, 0, width, axis=dim)
        edges[dim] = (
            lax.ppermute(last, axis, up),
            lax.ppermute(first, axis, [(b, a) for a, b in up]),
        )
    done = []
    for _, dim in sides:
        low, high = edges[dim]
        around = [(width, width) if d in done else (0, 0) for d in range(value.ndim)]
        value = jnp.concatenate([jnp.pad(low, around), value, jnp.pad(high, around)], axis=dim)
        done.append(dim)
    return value


STAGES = ("dev_0", "sec_0", "sec_1", "dev_1", "dev_2")


def shifted(value, axis):
    count = lax.axis_size(axis)
    pieces = [value]
    for shift in range(1, count):
        route = [(i, (i + shift) % count) for i in range(count)]
        pieces.append(lax.ppermute(value, axis, route))
    return pieces


def staged_gather(block, fillers):
    value = block
    done = []
    for stage, axis in enumerate(STAGES[:3]):
        pieces = shifted(value, axis)
        done.append(fillers[stage]())
        value = jnp.stack(pieces)
    value = value.reshape((-1,) + block.shape)
    pieces = shifted(value, STAGES[3])
    done.append(fillers[3]())
    gathered = jnp.stack([piece[..., :Q] for piece in pieces])
    summed = pieces[0][..., Q:]
    for piece in pieces[1:]:
        summed = summed + piece[..., Q:]
    gathered_pieces = shifted(gathered, STAGES[4])
    summed_pieces = shifted(summed, STAGES[4])
    done.append(fillers[4]())
    gathered = jnp.stack(gathered_pieces).reshape((-1,) + block.shape[:-1] + (Q,))
    summed = summed_pieces[0]
    for piece in summed_pieces[1:]:
        summed = summed + piece
    return gathered, summed, done


def group_slot(groups):
    coords = {}
    rest = groups
    for axis in reversed(SEC_DEV[:3]):
        count = lax.axis_size(axis)
        coords[axis] = rest % count
        rest = rest // count
    slot = jnp.zeros_like(groups)
    for axis in reversed(STAGES[:3]):
        count = lax.axis_size(axis)
        shift = (lax.axis_index(axis) - coords[axis]) % count
        slot = slot * count + shift
    return slot


def slot_of(boxes):
    coords = {}
    rest = boxes
    for axis in reversed(SEC_DEV):
        count = lax.axis_size(axis)
        coords[axis] = rest % count
        rest = rest // count
    slot = jnp.zeros_like(boxes)
    for axis in reversed(STAGES):
        count = lax.axis_size(axis)
        shift = (lax.axis_index(axis) - coords[axis]) % count
        slot = slot * count + shift
    return slot


TWO_OVER_PI = 0.6366197723675814
PIO2_1 = 1.5703125
PIO2_2 = 4.837512969970703125e-4
PIO2_3 = 7.54978995489188216e-8


def sincos(x):
    turns = jnp.round(x * TWO_OVER_PI)
    r = ((x - turns * PIO2_1) - turns * PIO2_2) - turns * PIO2_3
    z = r * r
    s = r + r * z * (-1.6666654611e-1 + z * (8.3321608736e-3 + z * -1.9515295891e-4))
    c = 1.0 - 0.5 * z + z * z * (
        4.166664568298827e-2 + z * (-1.388731625493765e-3 + z * 2.443315711809948e-5)
    )
    quadrant = turns.astype(jnp.int32) & 3
    swap = (quadrant & 1) == 1
    sin_v = jnp.where(swap, c, s)
    cos_v = jnp.where(swap, s, c)
    sin_v = jnp.where(quadrant >= 2, -sin_v, sin_v)
    cos_v = jnp.where((quadrant == 1) | (quadrant == 2), -cos_v, cos_v)
    return sin_v, cos_v


def _apply_body(scale, waves_ref, tgt_ref, src_ref, val_ref, out_ref):
    targets = tgt_ref[0]
    sources = src_ref[0]
    squared = None
    for axis in range(3):
        offset = targets[:, axis : axis + 1] - sources[axis : axis + 1, :]
        squared = offset * offset if squared is None else squared + offset * offset
    distance = jnp.sqrt(squared + SOFT * SOFT)
    amplitude = scale / distance
    dims = (((1,), (1,)), ((), ()))
    highest = lax.Precision.HIGHEST
    for f in range(out_ref.shape[1]):
        phase = waves_ref[f] * distance
        sin_v, cos_v = sincos(phase)
        real_kernel = amplitude * cos_v
        imag_kernel = amplitude * sin_v
        values = val_ref[0, f]
        real_part = lax.dot_general(values, real_kernel, dims, precision=highest, preferred_element_type=jnp.float32)
        imag_part = lax.dot_general(values, imag_kernel, dims, precision=highest, preferred_element_type=jnp.float32)
        out_ref[0, f, 0:1, :] = real_part[0:1] - imag_part[1:2]
        out_ref[0, f, 1:2, :] = real_part[1:2] + imag_part[0:1]


def apply_kernel(targets, sources, values, waves, scale):
    n, a, _ = targets.shape
    b = sources.shape[2]
    f = values.shape[1]
    return pl.pallas_call(
        functools.partial(_apply_body, scale),
        grid=(n,),
        in_specs=[
            pl.BlockSpec(memory_space=pltpu.SMEM),
            pl.BlockSpec((1, a, 3), lambda i: (i, 0, 0)),
            pl.BlockSpec((1, 3, b), lambda i: (i, 0, 0)),
            pl.BlockSpec((1, f, 2, b), lambda i: (i, 0, 0, 0)),
        ],
        out_specs=pl.BlockSpec((1, f, 2, a), lambda i: (i, 0, 0, 0)),
        out_shape=jax.ShapeDtypeStruct((n, f, 2, a), jnp.float32),
    )(waves, targets, sources, values)


def helmholtz(targets, sources, values, waves, scale):
    out = apply_kernel(
        jnp.swapaxes(targets, 1, 2), sources, jnp.swapaxes(values, 1, 2), waves, scale
    )
    return jnp.swapaxes(out, 1, 2)


def staged_sum(value):
    for axis in STAGES:
        count = lax.axis_size(axis)
        pieces = [value]
        for shift in range(1, count):
            route = [(i, (i + shift) % count) for i in range(count)]
            pieces.append(lax.ppermute(value, axis, route))
        stacked = jnp.stack(pieces)
        order = (lax.axis_index(axis) - jnp.arange(count, dtype=jnp.int32)) % count
        ordered = stacked[order]
        value = ordered[0]
        for j in range(1, count):
            value = value + ordered[j]
    return value


def device_body(
    sources,
    positions,
    weights,
    wavenumbers,
    directions,
    box_centers,
    group_centers,
    near_pairs,
    pair_counts,
    box_lists,
    group_lists,
):
    radius_box = 1.0 + 0.5 * LEAVES
    radius_group = 2.0 * radius_box
    device_index = lax.axis_index(SEC_DEV)
    weighted = sources * weights[None, None, :]
    packed = jnp.concatenate([weighted.reshape(2 * F, P_DEV), positions], axis=0)
    window = extended(packed, ((SEC_DEV, 1),), P_DEV)
    window_values = window[: 2 * F].reshape(2, F, 3 * LEAVES, LEAF)
    window_xyz = window[2 * F :].reshape(3, 3 * LEAVES, LEAF)
    local_xyz = positions.reshape(3, LEAVES, LEAF)
    targets = near_pairs[0, 0]
    anchors = near_pairs[0, 1]
    live_count = pair_counts[0]
    pair_ids = jnp.arange(PAIRS_MAX, dtype=jnp.int32)
    leaf_ids = jnp.arange(LEAVES, dtype=jnp.int32)
    live = (pair_ids < live_count).astype(jnp.float32)
    near_values = jnp.transpose(window_values[:, :, anchors], (2, 0, 1, 3)) * live[:, None, None, None]
    near_targets = jnp.transpose(local_xyz[:, targets], (1, 0, 2))
    near_sources = jnp.transpose(window_xyz[:, anchors], (1, 0, 2))
    chunk = -(-PAIRS_MAX // len(STAGES))

    def near_part(first):
        def run():
            picked = slice(first, min(first + chunk, PAIRS_MAX))
            return helmholtz(
                near_targets[picked], near_sources[picked], near_values[picked], wavenumbers, 1.0
            )

        return run

    near_runs = [near_part(k * chunk) for k in range(len(STAGES))]
    fillers = [lambda: [], lambda: [], lambda: []]
    fillers += [lambda: [run() for run in near_runs], lambda: []]
    own_center = lax.dynamic_index_in_dim(box_centers, device_index, 1, keepdims=False)
    own_proxies = own_center[:, None] + radius_box * directions
    own_multipole = helmholtz(
        own_proxies[None], positions[None], weighted[None], wavenumbers, radius_box
    )[0] / math.sqrt(P_DEV)
    parent = device_index // GROUP
    parent_proxies = (
        lax.dynamic_index_in_dim(group_centers, parent, 1, keepdims=False)[:, None]
        + radius_group * directions
    )
    source_groups = lax.dynamic_index_in_dim(group_lists, parent, 0, keepdims=False)
    contribution = helmholtz(
        parent_proxies[None], own_proxies[None], own_multipole[None], wavenumbers, radius_group
    )[0] / math.sqrt(GROUP * Q)
    gathered, summed, parts = staged_gather(
        jnp.concatenate([own_multipole, contribution], axis=2), fillers
    )
    blocks = jnp.concatenate([block for group in parts for block in group], axis=0)
    placing = (targets[:, None] == leaf_ids[None, :]).astype(jnp.float32)
    near_total = jnp.einsum(
        "srfa,sl->rfla", blocks, placing, precision=lax.Precision.HIGHEST
    ).reshape(2, F, P_DEV)
    source_boxes = box_lists[0]
    source_multipoles = summed[group_slot(source_groups)]
    source_proxies = box_centers[:, source_boxes][:, :, None] + radius_box * directions[:, None, :]
    incoming = helmholtz(
        jnp.broadcast_to(own_proxies, (source_boxes.shape[0],) + own_proxies.shape),
        jnp.transpose(source_proxies, (1, 0, 2)),
        gathered[slot_of(source_boxes)],
        wavenumbers,
        radius_box,
    ).sum(0) / math.sqrt(ML1 * Q)
    group_proxies = (
        group_centers[:, source_groups][:, :, None] + radius_group * directions[:, None, :]
    )
    group_local = helmholtz(
        jnp.broadcast_to(parent_proxies, (source_groups.shape[0],) + parent_proxies.shape),
        jnp.transpose(group_proxies, (1, 0, 2)),
        source_multipoles,
        wavenumbers,
        radius_group,
    ).sum(0) / math.sqrt(ML2 * Q)
    descended = helmholtz(
        own_proxies[None], parent_proxies[None], group_local[None], wavenumbers, radius_group
    )[0] / math.sqrt(Q)
    box_local = incoming + descended
    far_field = helmholtz(
        positions[None], own_proxies[None], box_local[None], wavenumbers, radius_box
    )[0] / math.sqrt(Q)
    result = 0.5 * sources + near_total / math.sqrt(LEAF * PAIRS_LEAF) + far_field
    real_sum = jnp.sum(sources[0] * result[0] + sources[1] * result[1], axis=-1)
    imag_sum = jnp.sum(sources[0] * result[1] - sources[1] * result[0], axis=-1)
    squares = jnp.sum(sources[0] * sources[0] + sources[1] * sources[1], axis=-1)
    sums = staged_sum(jnp.stack([real_sum, imag_sum, squares]))
    rayleigh = sums[:2] / (sums[2] + 1e-06)[None, :]
    return (result, rayleigh)


def solution(mesh):
    split = Mesh(mesh.devices.reshape(2, 4, 4, 4, 2), ("sec_0", "sec_1", "dev_0", "dev_1", "dev_2"))
    placed = (
        P(None, None, SEC_DEV),
        P(None, SEC_DEV),
        P(SEC_DEV),
        P(),
        P(),
        P(),
        P(),
        P(SEC_DEV, None, None),
        P(SEC_DEV),
        P(SEC_DEV, None),
        P(),
    )
    return jax.shard_map(
        device_body,
        mesh=split,
        in_specs=placed,
        out_specs=(P(None, None, SEC_DEV), P()),
        check_vma=False,
    )
```

```python
import functools
import math

import jax
import jax.numpy as jnp
from jax import lax
from jax.experimental import pallas as pl
from jax.experimental.pallas import tpu as pltpu
from jax.sharding import Mesh
from jax.sharding import PartitionSpec as P

LEAF = 128
LEAVES = 2
F = 8
Q = 128
PAIRS_LEAF = 5
ML1 = 4
ML2 = 2
GROUP = 8
P_DEV = 256
PAIRS_MAX = 10
SEC_DEV = ("sec_0", "sec_1", "dev_0", "dev_1", "dev_2")


SOFT = 0.1


def extended(value, sides, width):
    edges = {}
    for axis, dim in sides:
        devices, length = (lax.axis_size(axis), value.shape[dim])
        up = [(i, (i + 1) % devices) for i in range(devices - 1)]
        last = lax.slice_in_dim(value, length - width, length, axis=dim)
        first = lax.slice_in_dim(value, 0, width, axis=dim)
        edges[dim] = (
            lax.ppermute(last, axis, up),
            lax.ppermute(first, axis, [(b, a) for a, b in up]),
        )
    done = []
    for _, dim in sides:
        low, high = edges[dim]
        around = [(width, width) if d in done else (0, 0) for d in range(value.ndim)]
        value = jnp.concatenate([jnp.pad(low, around), value, jnp.pad(high, around)], axis=dim)
        done.append(dim)
    return value


STAGES = ("dev_0", "sec_0", "sec_1", "dev_1", "dev_2")


def shifted(value, axis):
    count = lax.axis_size(axis)
    pieces = [value]
    for shift in range(1, count):
        route = [(i, (i + shift) % count) for i in range(count)]
        pieces.append(lax.ppermute(value, axis, route))
    return pieces


def staged_gather(block, fillers):
    value = block
    done = []
    for stage, axis in enumerate(STAGES[:3]):
        pieces = shifted(value, axis)
        done.append(fillers[stage]())
        value = jnp.stack(pieces)
    value = value.reshape((-1,) + block.shape)
    pieces = shifted(value, STAGES[3])
    done.append(fillers[3]())
    gathered = jnp.stack([piece[..., :Q] for piece in pieces])
    summed = pieces[0][..., Q:]
    for piece in pieces[1:]:
        summed = summed + piece[..., Q:]
    gathered_pieces = shifted(gathered, STAGES[4])
    summed_pieces = shifted(summed, STAGES[4])
    done.append(fillers[4]())
    gathered = jnp.stack(gathered_pieces).reshape((-1,) + block.shape[:-1] + (Q,))
    summed = summed_pieces[0]
    for piece in summed_pieces[1:]:
        summed = summed + piece
    return gathered, summed, done


def group_slot(groups):
    coords = {}
    rest = groups
    for axis in reversed(SEC_DEV[:3]):
        count = lax.axis_size(axis)
        coords[axis] = rest % count
        rest = rest // count
    slot = jnp.zeros_like(groups)
    for axis in reversed(STAGES[:3]):
        count = lax.axis_size(axis)
        shift = (lax.axis_index(axis) - coords[axis]) % count
        slot = slot * count + shift
    return slot


def slot_of(boxes):
    coords = {}
    rest = boxes
    for axis in reversed(SEC_DEV):
        count = lax.axis_size(axis)
        coords[axis] = rest % count
        rest = rest // count
    slot = jnp.zeros_like(boxes)
    for axis in reversed(STAGES):
        count = lax.axis_size(axis)
        shift = (lax.axis_index(axis) - coords[axis]) % count
        slot = slot * count + shift
    return slot


TWO_OVER_PI = 0.6366197723675814
PIO2_1 = 1.5703125
PIO2_2 = 4.837512969970703125e-4
PIO2_3 = 7.54978995489188216e-8


def sincos(x):
    turns = jnp.round(x * TWO_OVER_PI)
    r = ((x - turns * PIO2_1) - turns * PIO2_2) - turns * PIO2_3
    z = r * r
    s = r + r * z * (-1.6666654611e-1 + z * (8.3321608736e-3 + z * -1.9515295891e-4))
    c = 1.0 - 0.5 * z + z * z * (
        4.166664568298827e-2 + z * (-1.388731625493765e-3 + z * 2.443315711809948e-5)
    )
    quadrant = turns.astype(jnp.int32) & 3
    swap = (quadrant & 1) == 1
    sin_v = jnp.where(swap, c, s)
    cos_v = jnp.where(swap, s, c)
    sin_v = jnp.where(quadrant >= 2, -sin_v, sin_v)
    cos_v = jnp.where((quadrant == 1) | (quadrant == 2), -cos_v, cos_v)
    return sin_v, cos_v


def _apply_body(scale, waves_ref, tgt_ref, src_ref, val_ref, out_ref):
    targets = tgt_ref[0]
    sources = src_ref[0]
    squared = None
    for axis in range(3):
        offset = targets[:, axis : axis + 1] - sources[axis : axis + 1, :]
        squared = offset * offset if squared is None else squared + offset * offset
    distance = jnp.sqrt(squared + SOFT * SOFT)
    amplitude = scale / distance
    dims = (((1,), (1,)), ((), ()))
    highest = lax.Precision.HIGHEST
    for f in range(out_ref.shape[1]):
        phase = waves_ref[f] * distance
        sin_v, cos_v = sincos(phase)
        real_kernel = amplitude * cos_v
        imag_kernel = amplitude * sin_v
        values = val_ref[0, f]
        real_part = lax.dot_general(values, real_kernel, dims, precision=highest, preferred_element_type=jnp.float32)
        imag_part = lax.dot_general(values, imag_kernel, dims, precision=highest, preferred_element_type=jnp.float32)
        out_ref[0, f, 0:1, :] = real_part[0:1] - imag_part[1:2]
        out_ref[0, f, 1:2, :] = real_part[1:2] + imag_part[0:1]


def apply_kernel(targets, sources, values, waves, scale):
    n, a, _ = targets.shape
    b = sources.shape[2]
    f = values.shape[1]
    return pl.pallas_call(
        functools.partial(_apply_body, scale),
        grid=(n,),
        in_specs=[
            pl.BlockSpec(memory_space=pltpu.SMEM),
            pl.BlockSpec((1, a, 3), lambda i: (i, 0, 0)),
            pl.BlockSpec((1, 3, b), lambda i: (i, 0, 0)),
            pl.BlockSpec((1, f, 2, b), lambda i: (i, 0, 0, 0)),
        ],
        out_specs=pl.BlockSpec((1, f, 2, a), lambda i: (i, 0, 0, 0)),
        out_shape=jax.ShapeDtypeStruct((n, f, 2, a), jnp.float32),
    )(waves, targets, sources, values)


def helmholtz(targets, sources, values, waves, scale):
    out = apply_kernel(
        jnp.swapaxes(targets, 1, 2), sources, jnp.swapaxes(values, 1, 2), waves, scale
    )
    return jnp.swapaxes(out, 1, 2)


def staged_sum(value):
    for axis in STAGES:
        count = lax.axis_size(axis)
        pieces = [value]
        for shift in range(1, count):
            route = [(i, (i + shift) % count) for i in range(count)]
            pieces.append(lax.ppermute(value, axis, route))
        stacked = jnp.stack(pieces)
        order = (lax.axis_index(axis) - jnp.arange(count, dtype=jnp.int32)) % count
        ordered = stacked[order]
        value = ordered[0]
        for j in range(1, count):
            value = value + ordered[j]
    return value


def device_body(
    sources,
    positions,
    weights,
    wavenumbers,
    directions,
    box_centers,
    group_centers,
    near_pairs,
    pair_counts,
    box_lists,
    group_lists,
):
    radius_box = 1.0 + 0.5 * LEAVES
    radius_group = 2.0 * radius_box
    device_index = lax.axis_index(SEC_DEV)
    weighted = sources * weights[None, None, :]
    packed = jnp.concatenate([weighted.reshape(2 * F, P_DEV), positions], axis=0)
    window = extended(packed, ((SEC_DEV, 1),), P_DEV)
    window_values = window[: 2 * F].reshape(2, F, 3 * LEAVES, LEAF)
    window_xyz = window[2 * F :].reshape(3, 3 * LEAVES, LEAF)
    local_xyz = positions.reshape(3, LEAVES, LEAF)
    targets = near_pairs[0, 0]
    anchors = near_pairs[0, 1]
    live_count = pair_counts[0]
    pair_ids = jnp.arange(PAIRS_MAX, dtype=jnp.int32)
    leaf_ids = jnp.arange(LEAVES, dtype=jnp.int32)
    live = (pair_ids < live_count).astype(jnp.float32)
    near_values = jnp.transpose(window_values[:, :, anchors], (2, 0, 1, 3)) * live[:, None, None, None]
    near_targets = jnp.transpose(local_xyz[:, targets], (1, 0, 2))
    near_sources = jnp.transpose(window_xyz[:, anchors], (1, 0, 2))
    chunk = -(-PAIRS_MAX // len(STAGES))

    def near_part(first, size=chunk):
        def run():
            picked = slice(first, min(first + size, PAIRS_MAX))
            return helmholtz(
                near_targets[picked], near_sources[picked], near_values[picked], wavenumbers, 1.0
            )

        return run

    near_runs = [near_part(k * chunk) for k in range(len(STAGES))]
    single = [near_part(chunk, 1), near_part(chunk + 1, 1), near_part(chunk + 2, PAIRS_MAX)]
    fillers = [lambda: [near_runs[0]()], lambda: [single[0]()], lambda: [single[1]()]]
    fillers += [lambda: [single[2]()], lambda: []]
    own_center = lax.dynamic_index_in_dim(box_centers, device_index, 1, keepdims=False)
    own_proxies = own_center[:, None] + radius_box * directions
    own_multipole = helmholtz(
        own_proxies[None], positions[None], weighted[None], wavenumbers, radius_box
    )[0] / math.sqrt(P_DEV)
    parent = device_index // GROUP
    parent_proxies = (
        lax.dynamic_index_in_dim(group_centers, parent, 1, keepdims=False)[:, None]
        + radius_group * directions
    )
    source_groups = lax.dynamic_index_in_dim(group_lists, parent, 0, keepdims=False)
    contribution = helmholtz(
        parent_proxies[None], own_proxies[None], own_multipole[None], wavenumbers, radius_group
    )[0] / math.sqrt(GROUP * Q)
    gathered, summed, parts = staged_gather(
        jnp.concatenate([own_multipole, contribution], axis=2), fillers
    )
    blocks = jnp.concatenate([block for group in parts for block in group], axis=0)
    placing = (targets[:, None] == leaf_ids[None, :]).astype(jnp.float32)
    near_total = jnp.einsum(
        "srfa,sl->rfla", blocks, placing, precision=lax.Precision.HIGHEST
    ).reshape(2, F, P_DEV)
    source_boxes = box_lists[0]
    source_multipoles = summed[group_slot(source_groups)]
    source_proxies = box_centers[:, source_boxes][:, :, None] + radius_box * directions[:, None, :]
    incoming = helmholtz(
        jnp.broadcast_to(own_proxies, (source_boxes.shape[0],) + own_proxies.shape),
        jnp.transpose(source_proxies, (1, 0, 2)),
        gathered[slot_of(source_boxes)],
        wavenumbers,
        radius_box,
    ).sum(0) / math.sqrt(ML1 * Q)
    group_proxies = (
        group_centers[:, source_groups][:, :, None] + radius_group * directions[:, None, :]
    )
    group_local = helmholtz(
        jnp.broadcast_to(parent_proxies, (source_groups.shape[0],) + parent_proxies.shape),
        jnp.transpose(group_proxies, (1, 0, 2)),
        source_multipoles,
        wavenumbers,
        radius_group,
    ).sum(0) / math.sqrt(ML2 * Q)
    descended = helmholtz(
        own_proxies[None], parent_proxies[None], group_local[None], wavenumbers, radius_group
    )[0] / math.sqrt(Q)
    box_local = incoming + descended
    far_field = helmholtz(
        positions[None], own_proxies[None], box_local[None], wavenumbers, radius_box
    )[0] / math.sqrt(Q)
    result = 0.5 * sources + near_total / math.sqrt(LEAF * PAIRS_LEAF) + far_field
    real_sum = jnp.sum(sources[0] * result[0] + sources[1] * result[1], axis=-1)
    imag_sum = jnp.sum(sources[0] * result[1] - sources[1] * result[0], axis=-1)
    squares = jnp.sum(sources[0] * sources[0] + sources[1] * sources[1], axis=-1)
    sums = staged_sum(jnp.stack([real_sum, imag_sum, squares]))
    rayleigh = sums[:2] / (sums[2] + 1e-06)[None, :]
    return (result, rayleigh)


def solution(mesh):
    split = Mesh(mesh.devices.reshape(2, 4, 4, 4, 2), ("sec_0", "sec_1", "dev_0", "dev_1", "dev_2"))
    placed = (
        P(None, None, SEC_DEV),
        P(None, SEC_DEV),
        P(SEC_DEV),
        P(),
        P(),
        P(),
        P(),
        P(SEC_DEV, None, None),
        P(SEC_DEV),
        P(SEC_DEV, None),
        P(),
    )
    return jax.shard_map(
        device_body,
        mesh=split,
        in_specs=placed,
        out_specs=(P(None, None, SEC_DEV), P()),
        check_vma=False,
    )
```
